32 devices in a mesh: grp: 2 (over y), gx: 16 (over z, x, core).
Axes of the slice: x: 2, y: 2, z: 4, core: 2. Of those that a mesh axis runs over, the one named last changes fastest.
Arguments:
- volume: float32 [512, 896], P(('grp', 'gx')), parts along dimension 0, may hold values from -45 to 45
- bank: float32 [8, 4096], P(None, 'gx'), may hold values from -43 to 43
- orient: int32 [8], replicated, may hold values from 0 to 47
- bank_id: int32 [8], replicated, may hold values from 0 to 7, each once
- counts: int32 [8], replicated, may hold values from 1 to 16
Outputs:
- fields: float32 [4, 512, 896], P(None, ('grp', 'gx')), parts along dimension 1
The draws below stay inside these ranges and needn't reach their ends.
There are 2 independent parts, one for each index of `grp`. The reference program is written for one: setup_inputs(seed, part) draws one part's arguments, and reference() takes and returns one part's arrays. A program takes and returns all parts, laid end to end along the dimension named above; an argument that names none is the same for every part. Nothing has to cross between parts.
Inputs may be any that keep to these rules, and one draw needn't show every extreme that they name: `bank_id`: each of the 8 base templates is named by exactly one list entry.
All inputs are finite; a program needn't handle non-finite values.
Results may differ from the reference program's by a relative error of at most 0.0003.
Values sent between devices are 32-bit elements; how exact they have to be, the bound alone decides.
No kernel may reach another device: no remote copies, remote signals or barrier semaphores. Data moves between devices by JAX's collectives and lax.ppermute only.
A program may use at most 64 MiB of HBM per device.

```python
import math
import jax
import jax.numpy as jnp
import numpy as np
from jax import lax

BY = 8
BZ = 112
TS = 16
NT = 8
FIELDS = 4
PER = 2
NX = 256


def draw_volume(key, part):
    keys_all = jax.random.split(jax.random.fold_in(key, 11), 3)
    columns = BY * BZ
    row_scale = jnp.exp(jax.random.uniform(keys_all[1], (NX, 1), jnp.float32, 0.0, math.log(3.2)))
    col_scale = jnp.exp(jax.random.uniform(keys_all[2], (1, columns), jnp.float32, 0.0, math.log(3.2)))
    noise = jnp.clip(jax.random.normal(keys_all[0], (NX, columns), jnp.float32), -4.0, 4.0)
    return noise * row_scale * col_scale


def draw_bank(key, part):
    keys_all = jax.random.split(jax.random.fold_in(key, 23), 2)
    voxels = TS * TS * TS
    voxel_scale = jnp.exp(jax.random.uniform(keys_all[1], (NT, voxels), jnp.float32, 0.0, math.log(10.0)))
    noise = jnp.clip(jax.random.normal(keys_all[0], (NT, voxels), jnp.float32), -4.0, 4.0)
    return noise * voxel_scale


def touch_ends(entries, own_key, low, largest):
    index_at = [jax.random.randint(jax.random.fold_in(own_key, axis), (), 0, length) for axis, length in enumerate(entries.shape)]
    widest = entries.shape.index(max(entries.shape))
    neighbour = index_at[:widest] + [(index_at[widest] + 1) % entries.shape[widest]] + index_at[widest + 1:]
    return entries.at[tuple(index_at)].set(low).at[tuple(neighbour)].set(largest)


def setup_inputs(seed: int = 0, part: int = 0) -> dict:
    seeds = jax.random.split(jax.random.key(seed), 6)
    part_splits = jax.random.split(jax.random.fold_in(seeds[5], part), 6)
    return {
        "volume": draw_volume(jax.random.fold_in(jax.random.fold_in(seeds[5], part), 71), part),
        "bank": draw_bank(jax.random.fold_in(seeds[5], 71), part),
        "orient": touch_ends(jax.random.randint(seeds[2], (NT,), 0, 48), jax.random.fold_in(seeds[2], 1), 0, 47).astype(jnp.int32),
        "bank_id": jax.random.permutation(seeds[3], NT).astype(jnp.int32),
        "counts": touch_ends(jax.random.randint(seeds[4], (NT,), 1, 17), jax.random.fold_in(seeds[4], 1), 1, 16).astype(jnp.int32),
    }


epsilon = 1e-05
sharpness = 80.0
AXIS_ORDERS = np.array([[0, 1, 2], [0, 2, 1], [1, 0, 2], [1, 2, 0], [2, 0, 1], [2, 1, 0]], np.int32)

def rotate_template(flat_base, orient_one):
    coords = jnp.arange(TS ** 3, dtype=jnp.int32)
    index_set = jnp.stack([coords // (TS * TS), coords // TS % TS, coords % TS])
    order_row = orient_one // 8
    flip_set = orient_one % 8
    picked = (jnp.arange(6, dtype=jnp.int32) == order_row).astype(jnp.int32)
    ordering = lax.optimization_barrier(jnp.sum(picked[:, None] * jnp.asarray(AXIS_ORDERS), axis=0))
    source = jnp.zeros_like(coords)
    for axis_num in range(3):
        select = (ordering[axis_num] == jnp.arange(3, dtype=jnp.int32)).astype(jnp.int32)
        chosen = lax.optimization_barrier(jnp.sum(select[:, None] * index_set, axis=0))
        flipped = flip_set // 2 ** axis_num % 2
        placed = chosen + flipped * (TS - 1 - 2 * chosen)
        source = source * TS + placed
    return flat_base[source]

def normalized_kernel(flat_base, orient_one):
    rotated = rotate_template(flat_base, orient_one)
    centered = rotated - jnp.mean(rotated)
    return centered / jnp.sqrt(jnp.sum(centered * centered) + epsilon)

def reference(volume, bank, orient, bank_id, counts):
    half = TS // 2
    grid = volume.reshape(NX, BY, BZ)
    padded = jnp.pad(grid, ((half, TS - half), (half, TS - half), (half, TS - half)))
    full_shape = padded.shape
    spectrum = jnp.fft.rfftn(padded)

    def one_template(entry):
        flat_base = bank[bank_id[entry]]
        kernel = normalized_kernel(flat_base, orient[entry]).reshape(TS, TS, TS)
        kernel_spec = jnp.fft.rfftn(kernel, s=full_shape)
        product = jnp.fft.irfftn(spectrum * jnp.conj(kernel_spec), s=full_shape)
        return product[:NX, :BY, :BZ]
    numer = lax.map(one_template, jnp.arange(NT, dtype=jnp.int32))
    squares = padded * padded
    for axis_num in range(3):
        window = [1, 1, 1]
        window[axis_num] = TS
        squares = lax.reduce_window(squares, jnp.array(0, squares.dtype), lax.add, tuple(window), (1, 1, 1), 'VALID')
    energy = squares[:NX, :BY, :BZ]
    scores = numer / jnp.sqrt(energy + epsilon)[None]
    weights = counts.astype(jnp.float32)
    weighted = weights[:, None, None, None] * jnp.exp(sharpness * scores)
    grouped = lax.optimization_barrier(jnp.sum(weighted.reshape(FIELDS, PER, NX, BY, BZ), axis=1))
    totals = lax.optimization_barrier(jnp.sum(weights.reshape(FIELDS, PER), axis=1))
    fields = jnp.log(grouped / totals[:, None, None, None])
    return fields.reshape(FIELDS, NX, BY * BZ)
```

```python
import jax
import jax.numpy as jnp
import numpy as np
from jax import lax
from jax.sharding import PartitionSpec as P

BY = 8
BZ = 112
TS = 16
NT = 8
FIELDS = 4
ZB = 16

epsilon = 1e-05
sharpness = 80.0
AXIS_ORDERS = np.array([[0, 1, 2], [0, 2, 1], [1, 0, 2], [1, 2, 0], [2, 0, 1], [2, 1, 0]], np.int32)


def extended(x, sides, width):
    for axis, dim in sides:
        size, length = (lax.axis_size(axis), x.shape[dim])
        up = [(i, (i + 1) % size) for i in range(size - 1)]
        down = [(j, i) for i, j in up]
        last = lax.slice_in_dim(x, length - width, length, axis=dim)
        leading = lax.slice_in_dim(x, 0, width, axis=dim)
        before = lax.ppermute(last, axis, up)
        after = lax.ppermute(leading, axis, down)
        x = jnp.concatenate([before, x, after], axis=dim)
    return x


def band_table(positions, targets, period):
    offset = (positions[:, None] - targets[None, :]) % period
    return (offset < TS).astype(jnp.float32)


def contract(letters, data, table):
    return jnp.einsum(letters, data, table, precision=lax.Precision.HIGHEST)


def expand(flag):
    return flag[:, None, None, None]


def rotated_kernels(bank_full, orient, bank_id):
    count = bank_full.shape[0]
    base = bank_full.reshape(count, TS, TS, TS)
    picked = jnp.zeros((orient.shape[0], TS, TS, TS), jnp.float32)
    for m in range(count):
        picked = picked + jnp.where(expand(bank_id == m), base[m][None], 0.0)
    flips = orient % 8
    for axis_num in range(3):
        bit = (flips // 2**axis_num) % 2 == 1
        picked = jnp.where(expand(bit), jnp.flip(picked, axis=axis_num + 1), picked)
    order_row = orient // 8
    rotated = jnp.zeros_like(picked)
    for row in range(AXIS_ORDERS.shape[0]):
        perm = (0,) + tuple(1 + int(p) for p in np.argsort(AXIS_ORDERS[row]))
        rotated = rotated + jnp.where(expand(order_row == row), jnp.transpose(picked, perm), 0.0)
    flat = rotated.reshape(rotated.shape[0], -1)
    centered = flat - jnp.mean(flat, axis=1, keepdims=True)
    norm = jnp.sqrt(jnp.sum(centered * centered, axis=1, keepdims=True) + epsilon)
    return (centered / norm).reshape(rotated.shape)


def toeplitz_rhs(kernels):
    nt = kernels.shape[0]
    c = np.arange(TS)[:, None, None]
    w = np.arange(TS + ZB)[None, :, None]
    zl = np.arange(ZB)[None, None, :]
    shift = jnp.asarray((w - zl == c).astype(np.float32))
    rhs = jnp.einsum("tabc,cwz->abwtz", kernels, shift, precision=lax.Precision.HIGHEST)
    return rhs.reshape(TS, 1, TS * (TS + ZB), nt * ZB)


def local(volume, bank, orient, bank_id, counts):
    rows_x = volume.shape[0]
    half = TS // 2
    nt = orient.shape[0]
    grid = volume.reshape(rows_x, BY, BZ)
    len_x = rows_x + TS
    len_y = BY + TS
    len_z = BZ + TS
    blocks = BZ // ZB
    gathered = lax.all_gather(bank, "gx", axis=1, tiled=True)
    kernels = rotated_kernels(gathered, orient, bank_id)
    rhs = toeplitz_rhs(kernels)
    field_in = extended(grid, (("gx", 0),), half)
    padded = jnp.pad(field_in, ((0, 0), (half, TS - half), (half, TS - half)))
    zwin = jnp.stack([padded[:, :, zb * ZB: zb * ZB + TS + ZB] for zb in range(blocks)], axis=2)
    cols = jnp.stack([zwin[:, b: b + BY] for b in range(TS)], axis=3)
    cols = cols[: len_x - 1].reshape(1, len_x - 1, BY * blocks, TS * (TS + ZB))
    numer = lax.conv_general_dilated(
        cols, rhs, (1, 1), "VALID", dimension_numbers=("NHWC", "HWIO", "NHWC"),
        precision=lax.Precision.HIGH,
    )
    numer = numer.reshape(rows_x, BY, blocks, nt, ZB)
    pos_x = jnp.arange(len_x, dtype=jnp.int32)
    out_x = jnp.arange(rows_x, dtype=jnp.int32)
    pos_y = half + jnp.arange(BY, dtype=jnp.int32)
    pos_z = half + jnp.arange(BZ, dtype=jnp.int32)
    squares = field_in * field_in
    energy = contract(
        "xyz,zn->xyn", squares, band_table(pos_z, jnp.arange(BZ, dtype=jnp.int32), len_z)
    )
    energy = contract(
        "xyn,ym->xmn", energy, band_table(pos_y, jnp.arange(BY, dtype=jnp.int32), len_y)
    )
    energy = contract("xmn,xl->lmn", energy, band_table(pos_x, out_x, len_x))
    energy = energy.reshape(rows_x, BY, blocks, 1, ZB)
    scores = numer / jnp.sqrt(energy + epsilon)
    weights = counts.astype(jnp.float32)
    weighted = weights[:, None] * jnp.exp(sharpness * scores)
    grouped = jnp.sum(weighted.reshape(rows_x, BY, blocks, FIELDS, nt // FIELDS, ZB), axis=4)
    totals = jnp.sum(weights.reshape(FIELDS, nt // FIELDS), axis=1)
    fields = jnp.log(grouped / totals[:, None])
    fields = jnp.transpose(fields, (3, 0, 1, 2, 4))
    return fields.reshape(FIELDS, rows_x, BY * BZ)


def solution(mesh):
    in_specs = (P(("grp", "gx"), None), P(None, "gx"), P(), P(), P())
    out_specs = P(None, ("grp", "gx"), None)
    return jax.shard_map(local, mesh=mesh, in_specs=in_specs, out_specs=out_specs, check_vma=False)
```

```python
import jax
import jax.numpy as jnp
import numpy as np
from jax import lax
from jax.sharding import PartitionSpec as P

BY = 8
BZ = 112
TS = 16
NT = 8
FIELDS = 4
ZB = 16

epsilon = 1e-05
sharpness = 80.0
AXIS_ORDERS = np.array([[0, 1, 2], [0, 2, 1], [1, 0, 2], [1, 2, 0], [2, 0, 1], [2, 1, 0]], np.int32)


def extended(x, sides, width):
    for axis, dim in sides:
        size, length = (lax.axis_size(axis), x.shape[dim])
        up = [(i, (i + 1) % size) for i in range(size - 1)]
        down = [(j, i) for i, j in up]
        last = lax.slice_in_dim(x, length - width, length, axis=dim)
        leading = lax.slice_in_dim(x, 0, width, axis=dim)
        before = lax.ppermute(last, axis, up)
        after = lax.ppermute(leading, axis, down)
        x = jnp.concatenate([before, x, after], axis=dim)
    return x


def band_table(positions, targets, period):
    offset = (positions[:, None] - targets[None, :]) % period
    return (offset < TS).astype(jnp.float32)


def contract(letters, data, table):
    return jnp.einsum(letters, data, table, precision=lax.Precision.HIGHEST)


def expand(flag):
    return flag[:, None, None, None]


def gather_planes(bank, axis):
    size = lax.axis_size(axis)
    me = lax.axis_index(axis)
    held = bank[None]
    step = 1
    while step < size:
        pairs = [(i, i ^ step) for i in range(size)]
        other = lax.ppermute(held, axis, pairs)
        low = (me // step) % 2 == 0
        held = jnp.where(low, jnp.concatenate([held, other], 0), jnp.concatenate([other, held], 0))
        step *= 2
    return held


def rotated_kernels(planes, orient, bank_id):
    count = planes.shape[1]
    picked = jnp.zeros((orient.shape[0], TS, TS, TS), jnp.float32)
    for m in range(count):
        base = planes[:, m, :].reshape(TS, TS, TS)
        picked = picked + jnp.where(expand(bank_id == m), base[None], 0.0)
    flips = orient % 8
    for axis_num in range(3):
        bit = (flips // 2**axis_num) % 2 == 1
        picked = jnp.where(expand(bit), jnp.flip(picked, axis=axis_num + 1), picked)
    order_row = orient // 8
    rotated = jnp.zeros_like(picked)
    for row in range(AXIS_ORDERS.shape[0]):
        perm = (0,) + tuple(1 + int(p) for p in np.argsort(AXIS_ORDERS[row]))
        rotated = rotated + jnp.where(expand(order_row == row), jnp.transpose(picked, perm), 0.0)
    flat = rotated.reshape(rotated.shape[0], -1)
    centered = flat - jnp.mean(flat, axis=1, keepdims=True)
    norm = jnp.sqrt(jnp.sum(centered * centered, axis=1, keepdims=True) + epsilon)
    return (centered / norm).reshape(rotated.shape)


def toeplitz_rhs(kernels):
    nt = kernels.shape[0]
    kt = jnp.transpose(kernels, (1, 2, 3, 0)).reshape(TS * TS, TS * nt)
    c = lax.broadcasted_iota(jnp.int32, (TS, nt, TS + ZB, nt, ZB), 0)
    t = lax.broadcasted_iota(jnp.int32, (TS, nt, TS + ZB, nt, ZB), 1)
    w = lax.broadcasted_iota(jnp.int32, (TS, nt, TS + ZB, nt, ZB), 2)
    t2 = lax.broadcasted_iota(jnp.int32, (TS, nt, TS + ZB, nt, ZB), 3)
    zl = lax.broadcasted_iota(jnp.int32, (TS, nt, TS + ZB, nt, ZB), 4)
    shift = ((w - zl == c) & (t == t2)).astype(jnp.float32).reshape(TS * nt, -1)
    rhs = jnp.dot(kt, shift, precision=lax.Precision.HIGHEST)
    return rhs.reshape(TS, 1, TS * (TS + ZB), nt * ZB)


def local(volume, bank, orient, bank_id, counts):
    rows_x = volume.shape[0]
    half = TS // 2
    nt = orient.shape[0]
    grid = volume.reshape(rows_x, BY, BZ)
    len_x = rows_x + TS
    len_y = BY + TS
    len_z = BZ + TS
    blocks = BZ // ZB
    planes = gather_planes(bank, "gx")
    kernels = rotated_kernels(planes, orient, bank_id)
    rhs = toeplitz_rhs(kernels)
    field_in = extended(grid, (("gx", 0),), half)
    padded = jnp.pad(field_in, ((0, 0), (half, TS - half), (half, TS - half)))
    zwin = jnp.stack([padded[: len_x - 1, :, zb * ZB: zb * ZB + TS + ZB] for zb in range(blocks)], axis=1)
    cols = jnp.concatenate([zwin[:, :, b: b + BY] for b in range(TS)], axis=3)
    cols = cols.reshape(1, len_x - 1, blocks * BY, TS * (TS + ZB))
    numer = lax.conv_general_dilated(
        cols, rhs, (1, 1), "VALID", dimension_numbers=("NHWC", "HWIO", "NHWC"),
        precision=lax.Precision.HIGH,
    )
    numer = numer.reshape(rows_x, blocks, BY, nt, ZB)
    pos_x = jnp.arange(len_x, dtype=jnp.int32)
    out_x = jnp.arange(rows_x, dtype=jnp.int32)
    pos_y = half + jnp.arange(BY, dtype=jnp.int32)
    pos_z = half + jnp.arange(BZ, dtype=jnp.int32)
    squares = field_in * field_in
    energy = contract(
        "xyz,zn->xyn", squares, band_table(pos_z, jnp.arange(BZ, dtype=jnp.int32), len_z)
    )
    energy = contract(
        "xyn,ym->xmn", energy, band_table(pos_y, jnp.arange(BY, dtype=jnp.int32), len_y)
    )
    energy = contract("xmn,xl->lmn", energy, band_table(pos_x, out_x, len_x))
    energy = jnp.transpose(energy.reshape(rows_x, BY, blocks, ZB), (0, 2, 1, 3))[:, :, :, None]
    scores = numer / jnp.sqrt(energy + epsilon)
    weights = counts.astype(jnp.float32)
    weighted = weights[:, None] * jnp.exp(sharpness * scores)
    grouped = jnp.sum(weighted.reshape(rows_x, blocks, BY, FIELDS, nt // FIELDS, ZB), axis=4)
    totals = jnp.sum(weights.reshape(FIELDS, nt // FIELDS), axis=1)
    fields = jnp.log(grouped / totals[:, None])
    fields = jnp.transpose(fields, (3, 0, 2, 1, 4))
    return fields.reshape(FIELDS, rows_x, BY * BZ)


def solution(mesh):
    in_specs = (P(("grp", "gx"), None), P(None, "gx"), P(), P(), P())
    out_specs = P(None, ("grp", "gx"), None)
    return jax.shard_map(local, mesh=mesh, in_specs=in_specs, out_specs=out_specs, check_vma=False)
```

```python
import jax
import jax.numpy as jnp
import numpy as np
from jax import lax
from jax.experimental import pallas as pl
from jax.experimental.pallas import tpu as pltpu
from jax.sharding import PartitionSpec as P

BY = 8
BZ = 112
TS = 16
NT = 8
FIELDS = 4
ZB = 16

epsilon = 1e-05
sharpness = 80.0
AXIS_ORDERS = np.array([[0, 1, 2], [0, 2, 1], [1, 0, 2], [1, 2, 0], [2, 0, 1], [2, 1, 0]], np.int32)


def extended(x, sides, width):
    for axis, dim in sides:
        size, length = (lax.axis_size(axis), x.shape[dim])
        up = [(i, (i + 1) % size) for i in range(size - 1)]
        down = [(j, i) for i, j in up]
        last = lax.slice_in_dim(x, length - width, length, axis=dim)
        leading = lax.slice_in_dim(x, 0, width, axis=dim)
        before = lax.ppermute(last, axis, up)
        after = lax.ppermute(leading, axis, down)
        x = jnp.concatenate([before, x, after], axis=dim)
    return x


def band_table(positions, targets, period):
    offset = (positions[:, None] - targets[None, :]) % period
    return (offset < TS).astype(jnp.float32)


def contract(letters, data, table):
    return jnp.einsum(letters, data, table, precision=lax.Precision.HIGHEST)


def expand(flag):
    return flag[:, None, None, None]


def gather_planes(bank, axis):
    size = lax.axis_size(axis)
    me = lax.axis_index(axis)
    held = bank[None]
    step = 1
    while step < size:
        pairs = [(i, i ^ step) for i in range(size)]
        other = lax.ppermute(held, axis, pairs)
        low = (me // step) % 2 == 0
        held = jnp.where(low, jnp.concatenate([held, other], 0), jnp.concatenate([other, held], 0))
        step *= 2
    return held


def rotated_kernels(planes, orient, bank_id):
    count = planes.shape[1]
    picked = jnp.zeros((orient.shape[0], TS, TS, TS), jnp.float32)
    for m in range(count):
        base = planes[:, m, :].reshape(TS, TS, TS)
        picked = picked + jnp.where(expand(bank_id == m), base[None], 0.0)
    flips = orient % 8
    for axis_num in range(3):
        bit = (flips // 2**axis_num) % 2 == 1
        picked = jnp.where(expand(bit), jnp.flip(picked, axis=axis_num + 1), picked)
    order_row = orient // 8
    rotated = jnp.zeros_like(picked)
    for row in range(AXIS_ORDERS.shape[0]):
        perm = (0,) + tuple(1 + int(p) for p in np.argsort(AXIS_ORDERS[row]))
        rotated = rotated + jnp.where(expand(order_row == row), jnp.transpose(picked, perm), 0.0)
    flat = rotated.reshape(rotated.shape[0], -1)
    centered = flat - jnp.mean(flat, axis=1, keepdims=True)
    norm = jnp.sqrt(jnp.sum(centered * centered, axis=1, keepdims=True) + epsilon)
    return (centered / norm).reshape(rotated.shape)


def toeplitz_rhs(kernels):
    nt = kernels.shape[0]
    kt = jnp.transpose(kernels, (1, 2, 3, 0)).reshape(TS * TS, TS * nt)
    dims = (TS, nt, TS + ZB, nt, ZB)
    c = lax.broadcasted_iota(jnp.int32, dims, 0)
    t = lax.broadcasted_iota(jnp.int32, dims, 1)
    w = lax.broadcasted_iota(jnp.int32, dims, 2)
    t2 = lax.broadcasted_iota(jnp.int32, dims, 3)
    zl = lax.broadcasted_iota(jnp.int32, dims, 4)
    shift = ((w - zl == c) & (t == t2)).astype(jnp.float32).reshape(TS * nt, TS + ZB, nt * ZB)
    rhs = jnp.einsum("rk,kwn->rwn", kt, shift, precision=lax.Precision.HIGHEST)
    return rhs.reshape(TS, 1, TS * (TS + ZB), nt * ZB)


def im2col_kernel(p_ref, o_ref):
    for zb in range(o_ref.shape[1]):
        for b in range(TS):
            o_ref[:, zb, :, b * (TS + ZB):(b + 1) * (TS + ZB)] = p_ref[:, b:b + BY, zb * ZB: zb * ZB + TS + ZB]


def im2col(padded, blocks):
    rows = padded.shape[0]
    return pl.pallas_call(
        im2col_kernel,
        out_shape=jax.ShapeDtypeStruct((rows, blocks, BY, TS * (TS + ZB)), jnp.float32),
        in_specs=[pl.BlockSpec(memory_space=pltpu.VMEM)],
        out_specs=pl.BlockSpec(memory_space=pltpu.VMEM),
    )(padded)


def local(volume, bank, orient, bank_id, counts):
    rows_x = volume.shape[0]
    half = TS // 2
    nt = orient.shape[0]
    grid = volume.reshape(rows_x, BY, BZ)
    len_x = rows_x + TS
    len_y = BY + TS
    len_z = BZ + TS
    blocks = BZ // ZB
    planes = gather_planes(bank, "gx")
    per = nt // FIELDS
    order = [k * per + p for p in range(per) for k in range(FIELDS)]
    kernels = rotated_kernels(planes, orient[np.array(order)], bank_id[np.array(order)])
    rhs = toeplitz_rhs(kernels)
    field_in = extended(grid, (("gx", 0),), half)
    padded = jnp.pad(field_in, ((0, 0), (half, TS - half), (half, TS - half)))
    cols = im2col(padded[: len_x - 1], blocks)
    cols = cols.reshape(1, len_x - 1, blocks * BY, TS * (TS + ZB))
    numer = lax.conv_general_dilated(
        cols, rhs, (1, 1), "VALID", dimension_numbers=("NHWC", "HWIO", "NHWC"),
        precision=lax.Precision.HIGH,
    )
    numer = numer.reshape(rows_x, blocks * BY, nt * ZB)
    pos_x = jnp.arange(len_x, dtype=jnp.int32)
    out_x = jnp.arange(rows_x, dtype=jnp.int32)
    pos_y = half + jnp.arange(BY, dtype=jnp.int32)
    pos_z = half + jnp.arange(BZ, dtype=jnp.int32)
    squares = field_in * field_in
    energy = contract(
        "xyz,zn->xyn", squares, band_table(pos_z, jnp.arange(BZ, dtype=jnp.int32), len_z)
    )
    energy = contract(
        "xyn,ym->xmn", energy, band_table(pos_y, jnp.arange(BY, dtype=jnp.int32), len_y)
    )
    energy = contract("xmn,xl->lmn", energy, band_table(pos_x, out_x, len_x))
    energy = jnp.transpose(energy.reshape(rows_x, BY, blocks, ZB), (0, 2, 1, 3))
    energy = jnp.tile(energy.reshape(rows_x, blocks * BY, ZB), (1, 1, nt))
    scores = numer / jnp.sqrt(energy + epsilon)
    weights = counts[np.array(order)].astype(jnp.float32)
    weighted = jnp.repeat(weights, ZB)[None, None] * jnp.exp(sharpness * scores)
    half_lanes = FIELDS * ZB
    grouped = weighted[:, :, :half_lanes]
    for p in range(1, per):
        grouped = grouped + weighted[:, :, p * half_lanes:(p + 1) * half_lanes]
    totals = weights[:FIELDS]
    for p in range(1, per):
        totals = totals + weights[p * FIELDS:(p + 1) * FIELDS]
    fields = jnp.log(grouped / jnp.repeat(totals, ZB)[None, None])
    fields = fields.reshape(rows_x, blocks, BY, FIELDS, ZB)
    fields = jnp.transpose(fields, (3, 0, 2, 1, 4))
    return fields.reshape(FIELDS, rows_x, BY * BZ)


def solution(mesh):
    in_specs = (P(("grp", "gx"), None), P(None, "gx"), P(), P(), P())
    out_specs = P(None, ("grp", "gx"), None)
    return jax.shard_map(local, mesh=mesh, in_specs=in_specs, out_specs=out_specs, check_vma=False)
```

```python
import jax
import jax.numpy as jnp
import numpy as np
from jax import lax
from jax.experimental import pallas as pl
from jax.experimental.pallas import tpu as pltpu
from jax.sharding import PartitionSpec as P

BY = 8
BZ = 112
TS = 16
NT = 8
FIELDS = 4
ZB = 16

epsilon = 1e-05
sharpness = 80.0
AXIS_ORDERS = np.array([[0, 1, 2], [0, 2, 1], [1, 0, 2], [1, 2, 0], [2, 0, 1], [2, 1, 0]], np.int32)


def extended(x, sides, width):
    for axis, dim in sides:
        size, length = (lax.axis_size(axis), x.shape[dim])
        up = [(i, (i + 1) % size) for i in range(size - 1)]
        down = [(j, i) for i, j in up]
        last = lax.slice_in_dim(x, length - width, length, axis=dim)
        leading = lax.slice_in_dim(x, 0, width, axis=dim)
        before = lax.ppermute(last, axis, up)
        after = lax.ppermute(leading, axis, down)
        x = jnp.concatenate([before, x, after], axis=dim)
    return x


def band_table(positions, targets, period):
    offset = (positions[:, None] - targets[None, :]) % period
    return (offset < TS).astype(jnp.float32)


def contract(letters, data, table):
    return jnp.einsum(letters, data, table, precision=lax.Precision.HIGHEST)


def expand(flag):
    return flag[:, None, None, None]


def gather_planes(bank, axis):
    size = lax.axis_size(axis)
    me = lax.axis_index(axis)
    held = bank[None]
    step = 1
    while step < size:
        pairs = [(i, i ^ step) for i in range(size)]
        other = lax.ppermute(held, axis, pairs)
        low = (me // step) % 2 == 0
        held = jnp.where(low, jnp.concatenate([held, other], 0), jnp.concatenate([other, held], 0))
        step *= 2
    return held


def rotated_kernels(planes, orient, bank_id):
    count = planes.shape[1]
    picked = jnp.zeros((orient.shape[0], TS, TS, TS), jnp.float32)
    for m in range(count):
        base = planes[:, m, :].reshape(TS, TS, TS)
        picked = picked + jnp.where(expand(bank_id == m), base[None], 0.0)
    flips = orient % 8
    for axis_num in range(3):
        bit = (flips // 2**axis_num) % 2 == 1
        picked = jnp.where(expand(bit), jnp.flip(picked, axis=axis_num + 1), picked)
    order_row = orient // 8
    rotated = jnp.zeros_like(picked)
    for row in range(AXIS_ORDERS.shape[0]):
        perm = (0,) + tuple(1 + int(p) for p in np.argsort(AXIS_ORDERS[row]))
        rotated = rotated + jnp.where(expand(order_row == row), jnp.transpose(picked, perm), 0.0)
    flat = rotated.reshape(rotated.shape[0], -1)
    centered = flat - jnp.mean(flat, axis=1, keepdims=True)
    norm = jnp.sqrt(jnp.sum(centered * centered, axis=1, keepdims=True) + epsilon)
    return (centered / norm).reshape(rotated.shape)


def toeplitz_rhs(kernels):
    nt = kernels.shape[0]
    kt = jnp.transpose(kernels, (1, 2, 0, 3)).reshape(TS * TS, nt * TS)
    spread = jnp.pad(kt, ((0, 0), (ZB - 1, TS + ZB - ZB)))
    lanes = np.arange(nt * ZB) % ZB
    pieces = []
    for w in range(TS + ZB):
        keep = (lanes + w - (ZB - 1) >= 0) & (lanes + w - (ZB - 1) < TS)
        pieces.append(jnp.where(jnp.asarray(keep)[None], spread[:, w: w + nt * ZB], 0.0))
    rhs = jnp.stack(pieces, axis=1)
    return rhs.reshape(TS, 1, TS * (TS + ZB), nt * ZB)


def im2col_kernel(p_ref, o_ref):
    def body(y, carry):
        for zb in range(o_ref.shape[0]):
            for b in range(TS):
                o_ref[zb, y, :, b * (TS + ZB):(b + 1) * (TS + ZB)] = p_ref[y + b, :, zb * ZB: zb * ZB + TS + ZB]
        return carry
    lax.fori_loop(0, BY, body, 0)


def im2col(padded_t, blocks):
    rows = padded_t.shape[1]
    return pl.pallas_call(
        im2col_kernel,
        out_shape=jax.ShapeDtypeStruct((blocks, BY, rows, TS * (TS + ZB)), jnp.float32),
        in_specs=[pl.BlockSpec(memory_space=pltpu.VMEM)],
        out_specs=pl.BlockSpec(memory_space=pltpu.VMEM),
    )(padded_t)


def reorder(values, order):
    return jnp.concatenate([values[i: i + 1] for i in order])


def local(volume, bank, orient, bank_id, counts):
    rows_x = volume.shape[0]
    half = TS // 2
    nt = orient.shape[0]
    grid = volume.reshape(rows_x, BY, BZ)
    len_x = rows_x + TS
    len_y = BY + TS
    len_z = BZ + TS
    blocks = BZ // ZB
    planes = gather_planes(bank, "gx")
    per = nt // FIELDS
    order = [k * per + p for p in range(per) for k in range(FIELDS)]
    kernels = rotated_kernels(planes, reorder(orient, order), reorder(bank_id, order))
    rhs = toeplitz_rhs(kernels)
    field_in = extended(grid, (("gx", 0),), half)
    padded = jnp.pad(field_in, ((0, 0), (half, TS - half), (half, TS - half)))
    cols = im2col(jnp.transpose(padded[: len_x - 1], (1, 0, 2)), blocks)
    cols = cols.reshape(1, blocks * BY, len_x - 1, TS * (TS + ZB))
    numer = lax.conv_general_dilated(
        cols, rhs, (1, 1), "VALID",
        dimension_numbers=lax.ConvDimensionNumbers((0, 3, 2, 1), (3, 2, 0, 1), (0, 3, 1, 2)),
        precision=lax.Precision.HIGH,
    )
    numer = numer.reshape(rows_x, blocks * BY, nt * ZB)
    pos_x = jnp.arange(len_x, dtype=jnp.int32)
    out_x = jnp.arange(rows_x, dtype=jnp.int32)
    pos_y = half + jnp.arange(BY, dtype=jnp.int32)
    pos_z = half + jnp.arange(BZ, dtype=jnp.int32)
    squares = field_in * field_in
    energy = contract(
        "xyz,zn->xyn", squares, band_table(pos_z, jnp.arange(BZ, dtype=jnp.int32), len_z)
    )
    energy = contract(
        "xyn,ym->xmn", energy, band_table(pos_y, jnp.arange(BY, dtype=jnp.int32), len_y)
    )
    energy = contract("xmn,xl->lmn", energy, band_table(pos_x, out_x, len_x))
    energy = jnp.transpose(jnp.flip(energy.reshape(rows_x, BY, blocks, ZB), axis=3), (0, 2, 1, 3))
    energy = jnp.tile(energy.reshape(rows_x, blocks * BY, ZB), (1, 1, nt))
    scores = numer / jnp.sqrt(energy + epsilon)
    weights = reorder(counts, order).astype(jnp.float32)
    weighted = jnp.repeat(weights, ZB)[None, None] * jnp.exp(sharpness * scores)
    half_lanes = FIELDS * ZB
    grouped = weighted[:, :, :half_lanes]
    for p in range(1, per):
        grouped = grouped + weighted[:, :, p * half_lanes:(p + 1) * half_lanes]
    totals = weights[:FIELDS]
    for p in range(1, per):
        totals = totals + weights[p * FIELDS:(p + 1) * FIELDS]
    fields = jnp.log(grouped / jnp.repeat(totals, ZB)[None, None])
    fields = fields.reshape(rows_x, blocks, BY, FIELDS, ZB)
    fields = jnp.transpose(jnp.flip(fields, axis=4), (3, 0, 2, 1, 4))
    return fields.reshape(FIELDS, rows_x, BY * BZ)


def solution(mesh):
    in_specs = (P(("grp", "gx"), None), P(None, "gx"), P(), P(), P())
    out_specs = P(None, ("grp", "gx"), None)
    return jax.shard_map(local, mesh=mesh, in_specs=in_specs, out_specs=out_specs, check_vma=False)
```

```python
import jax
import jax.numpy as jnp
import numpy as np
from jax import lax
from jax.experimental import pallas as pl
from jax.experimental.pallas import tpu as pltpu
from jax.sharding import PartitionSpec as P

BY = 8
BZ = 112
TS = 16
NT = 8
FIELDS = 4
ZB = 16

epsilon = 1e-05
sharpness = 80.0
AXIS_ORDERS = np.array([[0, 1, 2], [0, 2, 1], [1, 0, 2], [1, 2, 0], [2, 0, 1], [2, 1, 0]], np.int32)


def extended(x, sides, width):
    for axis, dim in sides:
        size, length = (lax.axis_size(axis), x.shape[dim])
        up = [(i, (i + 1) % size) for i in range(size - 1)]
        down = [(j, i) for i, j in up]
        last = lax.slice_in_dim(x, length - width, length, axis=dim)
        leading = lax.slice_in_dim(x, 0, width, axis=dim)
        before = lax.ppermute(last, axis, up)
        after = lax.ppermute(leading, axis, down)
        x = jnp.concatenate([before, x, after], axis=dim)
    return x


def band_table(positions, targets, period):
    offset = (positions[:, None] - targets[None, :]) % period
    return (offset < TS).astype(jnp.float32)


def contract(letters, data, table):
    return jnp.einsum(letters, data, table, precision=lax.Precision.HIGHEST)


def expand(flag):
    return flag[:, None, None, None]


def gather_planes(bank, axis):
    size = lax.axis_size(axis)
    me = lax.axis_index(axis)
    held = bank[None]
    step = 1
    while step < size:
        pairs = [(i, i ^ step) for i in range(size)]
        other = lax.ppermute(held, axis, pairs)
        low = (me // step) % 2 == 0
        held = jnp.where(low, jnp.concatenate([held, other], 0), jnp.concatenate([other, held], 0))
        step *= 2
    return held


def rotated_kernels(planes, orient, bank_id):
    count = planes.shape[1]
    picked = jnp.zeros((orient.shape[0], TS, TS, TS), jnp.float32)
    for m in range(count):
        base = planes[:, m, :].reshape(TS, TS, TS)
        picked = picked + jnp.where(expand(bank_id == m), base[None], 0.0)
    flips = orient % 8
    for axis_num in range(3):
        bit = (flips // 2**axis_num) % 2 == 1
        picked = jnp.where(expand(bit), jnp.flip(picked, axis=axis_num + 1), picked)
    order_row = orient // 8
    rotated = jnp.zeros_like(picked)
    for row in range(AXIS_ORDERS.shape[0]):
        perm = (0,) + tuple(1 + int(p) for p in np.argsort(AXIS_ORDERS[row]))
        rotated = rotated + jnp.where(expand(order_row == row), jnp.transpose(picked, perm), 0.0)
    flat = rotated.reshape(rotated.shape[0], -1)
    centered = flat - jnp.mean(flat, axis=1, keepdims=True)
    norm = jnp.sqrt(jnp.sum(centered * centered, axis=1, keepdims=True) + epsilon)
    return (centered / norm).reshape(rotated.shape)


def toeplitz_rhs(kernels):
    nt = kernels.shape[0]
    per = nt // FIELDS
    kt = kernels.reshape(FIELDS, per, TS, TS, TS)
    kt = jnp.transpose(kt, (2, 3, 1, 0, 4)).reshape(TS * TS, TS * nt)
    dims = (TS + ZB, nt, TS, nt, ZB)
    w = lax.broadcasted_iota(jnp.int32, dims, 0)
    t = lax.broadcasted_iota(jnp.int32, dims, 1)
    c = lax.broadcasted_iota(jnp.int32, dims, 2)
    t2 = lax.broadcasted_iota(jnp.int32, dims, 3)
    zl = lax.broadcasted_iota(jnp.int32, dims, 4)
    shift = ((w - zl == c) & (t == t2)).astype(jnp.float32).reshape(TS + ZB, TS * nt, nt * ZB)
    rhs = jnp.einsum("rk,wkn->rwn", kt, shift, precision=lax.Precision.HIGHEST)
    return rhs.reshape(TS, 1, TS * (TS + ZB), nt * ZB)


def im2col_kernel(p_ref, o_ref):
    def body(y, carry):
        for zb in range(o_ref.shape[0]):
            for b in range(TS):
                o_ref[zb, y, :, b * (TS + ZB):(b + 1) * (TS + ZB)] = p_ref[y + b, :, zb * ZB: zb * ZB + TS + ZB]
        return carry
    lax.fori_loop(0, BY, body, 0)


def im2col(padded_t, blocks):
    rows = padded_t.shape[1]
    return pl.pallas_call(
        im2col_kernel,
        out_shape=jax.ShapeDtypeStruct((blocks, BY, rows, TS * (TS + ZB)), jnp.float32),
        in_specs=[pl.BlockSpec(memory_space=pltpu.VMEM)],
        out_specs=pl.BlockSpec(memory_space=pltpu.VMEM),
    )(padded_t)


def local(volume, bank, orient, bank_id, counts):
    rows_x = volume.shape[0]
    half = TS // 2
    nt = orient.shape[0]
    grid = volume.reshape(rows_x, BY, BZ)
    len_x = rows_x + TS
    len_y = BY + TS
    len_z = BZ + TS
    blocks = BZ // ZB
    planes = gather_planes(bank, "gx")
    per = nt // FIELDS
    kernels = rotated_kernels(planes, orient, bank_id)
    rhs = toeplitz_rhs(kernels)
    field_in = extended(grid, (("gx", 0),), half)
    padded = jnp.pad(field_in, ((0, 0), (half, TS - half), (half, TS - half)))
    cols = im2col(jnp.transpose(padded[: len_x - 1], (1, 0, 2)), blocks)
    cols = cols.reshape(1, blocks * BY, len_x - 1, TS * (TS + ZB))
    numer = lax.conv_general_dilated(
        cols, rhs, (1, 1), "VALID",
        dimension_numbers=lax.ConvDimensionNumbers((0, 3, 2, 1), (3, 2, 0, 1), (0, 3, 1, 2)),
        precision=lax.Precision.HIGH,
    )
    numer = numer.reshape(rows_x, blocks * BY, nt * ZB)
    pos_x = jnp.arange(len_x, dtype=jnp.int32)
    out_x = jnp.arange(rows_x, dtype=jnp.int32)
    pos_y = half + jnp.arange(BY, dtype=jnp.int32)
    pos_z = half + jnp.arange(BZ, dtype=jnp.int32)
    squares = field_in * field_in
    energy = contract(
        "xyz,zn->xyn", squares, band_table(pos_z, jnp.arange(BZ, dtype=jnp.int32), len_z)
    )
    energy = contract(
        "xyn,ym->xmn", energy, band_table(pos_y, jnp.arange(BY, dtype=jnp.int32), len_y)
    )
    energy = contract("xmn,xl->lmn", energy, band_table(pos_x, out_x, len_x))
    energy = jnp.transpose(energy.reshape(rows_x, BY, blocks, ZB), (0, 2, 1, 3))
    energy = jnp.tile(energy.reshape(rows_x, blocks * BY, ZB), (1, 1, nt))
    scores = numer / jnp.sqrt(energy + epsilon)
    weights = jnp.transpose(counts.astype(jnp.float32).reshape(FIELDS, per)).reshape(nt)
    weighted = jnp.repeat(weights, ZB)[None, None] * jnp.exp(sharpness * scores)
    half_lanes = FIELDS * ZB
    grouped = weighted[:, :, :half_lanes]
    for p in range(1, per):
        grouped = grouped + weighted[:, :, p * half_lanes:(p + 1) * half_lanes]
    totals = weights[:FIELDS]
    for p in range(1, per):
        totals = totals + weights[p * FIELDS:(p + 1) * FIELDS]
    fields = jnp.log(grouped / jnp.repeat(totals, ZB)[None, None])
    fields = fields.reshape(rows_x, blocks, BY, FIELDS, ZB)
    fields = jnp.transpose(fields, (3, 0, 2, 1, 4))
    return fields.reshape(FIELDS, rows_x, BY * BZ)


def solution(mesh):
    in_specs = (P(("grp", "gx"), None), P(None, "gx"), P(), P(), P())
    out_specs = P(None, ("grp", "gx"), None)
    return jax.shard_map(local, mesh=mesh, in_specs=in_specs, out_specs=out_specs, check_vma=False)
```

```python
import jax
import jax.numpy as jnp
import numpy as np
from jax import lax
from jax.experimental import pallas as pl
from jax.experimental.pallas import tpu as pltpu
from jax.sharding import PartitionSpec as P

BY = 8
BZ = 112
TS = 16
NT = 8
FIELDS = 4
ZB = 16

epsilon = 1e-05
sharpness = 80.0
AXIS_ORDERS = np.array([[0, 1, 2], [0, 2, 1], [1, 0, 2], [1, 2, 0], [2, 0, 1], [2, 1, 0]], np.int32)


def extended(x, sides, width):
    for axis, dim in sides:
        size, length = (lax.axis_size(axis), x.shape[dim])
        up = [(i, (i + 1) % size) for i in range(size - 1)]
        down = [(j, i) for i, j in up]
        last = lax.slice_in_dim(x, length - width, length, axis=dim)
        leading = lax.slice_in_dim(x, 0, width, axis=dim)
        before = lax.ppermute(last, axis, up)
        after = lax.ppermute(leading, axis, down)
        x = jnp.concatenate([before, x, after], axis=dim)
    return x


def band_table(positions, targets, period):
    offset = (positions[:, None] - targets[None, :]) % period
    return (offset < TS).astype(jnp.float32)


def contract(letters, data, table):
    return jnp.einsum(letters, data, table, precision=lax.Precision.HIGHEST)


def expand(flag):
    return flag[:, None, None, None]


def gather_planes(bank, axis):
    size = lax.axis_size(axis)
    me = lax.axis_index(axis)
    held = bank[None]
    step = 1
    while step < size:
        radix = min(4, size // step)
        digit = (me // step) % radix
        blocks = [held] + [
            lax.ppermute(held, axis, [(i, i ^ (s * step)) for i in range(size)]) for s in range(1, radix)
        ]
        placed = []
        for d in range(radix):
            value = jnp.zeros_like(held)
            for s in range(radix):
                value = value + jnp.where((digit ^ s) == d, blocks[s], 0.0)
            placed.append(value)
        held = jnp.concatenate(placed, 0)
        step *= radix
    return held


def rotated_kernels(planes, orient, bank_id):
    count = planes.shape[1]
    picked = jnp.zeros((orient.shape[0], TS, TS, TS), jnp.float32)
    for m in range(count):
        base = planes[:, m, :].reshape(TS, TS, TS)
        picked = picked + jnp.where(expand(bank_id == m), base[None], 0.0)
    flips = orient % 8
    for axis_num in range(3):
        bit = (flips // 2**axis_num) % 2 == 1
        picked = jnp.where(expand(bit), jnp.flip(picked, axis=axis_num + 1), picked)
    order_row = orient // 8
    rotated = jnp.zeros_like(picked)
    for row in range(AXIS_ORDERS.shape[0]):
        perm = (0,) + tuple(1 + int(p) for p in np.argsort(AXIS_ORDERS[row]))
        rotated = rotated + jnp.where(expand(order_row == row), jnp.transpose(picked, perm), 0.0)
    flat = rotated.reshape(rotated.shape[0], -1)
    centered = flat - jnp.mean(flat, axis=1, keepdims=True)
    norm = jnp.sqrt(jnp.sum(centered * centered, axis=1, keepdims=True) + epsilon)
    return (centered / norm).reshape(rotated.shape)


def toeplitz_rhs(kernels):
    nt = kernels.shape[0]
    per = nt // FIELDS
    kt = kernels.reshape(FIELDS, per, TS, TS, TS)
    kt = jnp.transpose(kt, (2, 3, 1, 0, 4)).reshape(TS * TS, TS * nt)
    dims = (TS + ZB, TS * nt, nt * ZB)
    w = lax.broadcasted_iota(jnp.int32, dims, 0)
    k = lax.broadcasted_iota(jnp.int32, dims, 1)
    n = lax.broadcasted_iota(jnp.int32, dims, 2)
    shift = ((w - n % ZB == k % TS) & (k // TS == n // ZB)).astype(jnp.float32)
    rhs = jnp.einsum("rk,wkn->rwn", kt, shift, precision=lax.Precision.HIGHEST)
    return rhs.reshape(TS, 1, TS * (TS + ZB), nt * ZB)


def im2col_kernel(p_ref, o_ref):
    def body(y, carry):
        for zb in range(o_ref.shape[0]):
            for b in range(TS):
                o_ref[zb, y, :, b * (TS + ZB):(b + 1) * (TS + ZB)] = p_ref[y + b, :, zb * ZB: zb * ZB + TS + ZB]
        return carry
    lax.fori_loop(0, BY, body, 0)


def im2col(padded_t, blocks):
    rows = padded_t.shape[1]
    return pl.pallas_call(
        im2col_kernel,
        out_shape=jax.ShapeDtypeStruct((blocks, BY, rows, TS * (TS + ZB)), jnp.float32),
        in_specs=[pl.BlockSpec(memory_space=pltpu.VMEM)],
        out_specs=pl.BlockSpec(memory_space=pltpu.VMEM),
        cost_estimate=pl.CostEstimate(flops=0, transcendentals=0, bytes_accessed=4 * blocks * BY * rows * TS * (TS + ZB)),
    )(padded_t)


def local(volume, bank, orient, bank_id, counts):
    rows_x = volume.shape[0]
    half = TS // 2
    nt = orient.shape[0]
    grid = volume.reshape(rows_x, BY, BZ)
    len_x = rows_x + TS
    len_y = BY + TS
    len_z = BZ + TS
    blocks = BZ // ZB
    planes = gather_planes(bank, "gx")
    per = nt // FIELDS
    kernels = rotated_kernels(planes, orient, bank_id)
    rhs = toeplitz_rhs(kernels)
    field_in = extended(grid, (("gx", 0),), half)
    padded = jnp.pad(field_in, ((0, 0), (half, TS - half), (half, TS - half)))
    cols = im2col(jnp.transpose(padded[: len_x - 1], (1, 0, 2)), blocks)
    cols = cols.reshape(1, blocks * BY, len_x - 1, TS * (TS + ZB))
    numer = lax.conv_general_dilated(
        cols, rhs, (1, 1), "VALID",
        dimension_numbers=lax.ConvDimensionNumbers((0, 3, 2, 1), (3, 2, 0, 1), (0, 3, 1, 2)),
        precision=lax.Precision.HIGH,
    )
    numer = numer.reshape(rows_x, blocks * BY, nt * ZB)
    pos_x = jnp.arange(len_x, dtype=jnp.int32)
    out_x = jnp.arange(rows_x, dtype=jnp.int32)
    pos_y = half + jnp.arange(BY, dtype=jnp.int32)
    pos_z = half + jnp.arange(BZ, dtype=jnp.int32)
    squares = field_in * field_in
    energy = contract(
        "xyz,zn->xyn", squares, band_table(pos_z, jnp.arange(BZ, dtype=jnp.int32), len_z)
    )
    energy = contract(
        "xyn,ym->xmn", energy, band_table(pos_y, jnp.arange(BY, dtype=jnp.int32), len_y)
    )
    energy = contract("xmn,xl->lmn", energy, band_table(pos_x, out_x, len_x))
    energy = jnp.transpose(energy.reshape(rows_x, BY, blocks, ZB), (0, 2, 1, 3))
    energy = jnp.tile(energy.reshape(rows_x, blocks * BY, ZB), (1, 1, nt))
    scores = numer / jnp.sqrt(energy + epsilon)
    weights = jnp.transpose(counts.astype(jnp.float32).reshape(FIELDS, per)).reshape(nt)
    weighted = jnp.repeat(weights, ZB)[None, None] * jnp.exp(sharpness * scores)
    half_lanes = FIELDS * ZB
    grouped = weighted[:, :, :half_lanes]
    for p in range(1, per):
        grouped = grouped + weighted[:, :, p * half_lanes:(p + 1) * half_lanes]
    totals = weights[:FIELDS]
    for p in range(1, per):
        totals = totals + weights[p * FIELDS:(p + 1) * FIELDS]
    fields = jnp.log(grouped / jnp.repeat(totals, ZB)[None, None])
    fields = fields.reshape(rows_x, blocks, BY, FIELDS, ZB)
    fields = jnp.transpose(fields, (3, 0, 2, 1, 4))
    return fields.reshape(FIELDS, rows_x, BY * BZ)


def solution(mesh):
    in_specs = (P(("grp", "gx"), None), P(None, "gx"), P(), P(), P())
    out_specs = P(None, ("grp", "gx"), None)
    return jax.shard_map(local, mesh=mesh, in_specs=in_specs, out_specs=out_specs, check_vma=False)
```

```python
import jax
import jax.numpy as jnp
import numpy as np
from jax import lax
from jax.experimental import pallas as pl
from jax.experimental.pallas import tpu as pltpu
from jax.sharding import PartitionSpec as P

BY = 8
BZ = 112
TS = 16
NT = 8
FIELDS = 4
ZB = 16

epsilon = 1e-05
sharpness = 80.0
AXIS_ORDERS = np.array([[0, 1, 2], [0, 2, 1], [1, 0, 2], [1, 2, 0], [2, 0, 1], [2, 1, 0]], np.int32)


def extended(x, sides, width):
    for axis, dim in sides:
        size, length = (lax.axis_size(axis), x.shape[dim])
        up = [(i, (i + 1) % size) for i in range(size - 1)]
        down = [(j, i) for i, j in up]
        last = lax.slice_in_dim(x, length - width, length, axis=dim)
        leading = lax.slice_in_dim(x, 0, width, axis=dim)
        before = lax.ppermute(last, axis, up)
        after = lax.ppermute(leading, axis, down)
        x = jnp.concatenate([before, x, after], axis=dim)
    return x


def band_table(positions, targets, period):
    offset = (positions[:, None] - targets[None, :]) % period
    return (offset < TS).astype(jnp.float32)


def contract(letters, data, table):
    return jnp.einsum(letters, data, table, precision=lax.Precision.HIGHEST)


def expand(flag):
    return flag[:, None, None, None]


def gather_planes(bank, axis):
    size = lax.axis_size(axis)
    me = lax.axis_index(axis)
    held = bank[None]
    step = 1
    while step < size:
        radix = min(4, size // step)
        digit = (me // step) % radix
        blocks = [held] + [
            lax.ppermute(held, axis, [(i, i ^ (s * step)) for i in range(size)]) for s in range(1, radix)
        ]
        placed = []
        for d in range(radix):
            value = jnp.zeros_like(held)
            for s in range(radix):
                value = value + jnp.where((digit ^ s) == d, blocks[s], 0.0)
            placed.append(value)
        held = jnp.concatenate(placed, 0)
        step *= radix
    return held


def rotated_kernels(planes, orient, bank_id):
    count = planes.shape[1]
    choice = (bank_id[:, None] == jnp.arange(count, dtype=jnp.int32)[None, :]).astype(jnp.float32)
    picked = jnp.einsum("tm,amv->tav", choice, planes, precision=lax.Precision.HIGHEST)
    picked = picked.reshape(orient.shape[0], TS, TS, TS)
    flips = orient % 8
    for axis_num in range(3):
        bit = (flips // 2**axis_num) % 2 == 1
        picked = jnp.where(expand(bit), jnp.flip(picked, axis=axis_num + 1), picked)
    order_row = orient // 8
    rotated = jnp.zeros_like(picked)
    for row in range(AXIS_ORDERS.shape[0]):
        perm = (0,) + tuple(1 + int(p) for p in np.argsort(AXIS_ORDERS[row]))
        rotated = rotated + jnp.where(expand(order_row == row), jnp.transpose(picked, perm), 0.0)
    flat = rotated.reshape(rotated.shape[0], -1)
    centered = flat - jnp.mean(flat, axis=1, keepdims=True)
    norm = jnp.sqrt(jnp.sum(centered * centered, axis=1, keepdims=True) + epsilon)
    return (centered / norm).reshape(rotated.shape)


def toeplitz_rhs(kernels):
    nt = kernels.shape[0]
    per = nt // FIELDS
    dims = (TS + ZB, TS * nt, nt * ZB)
    w = lax.broadcasted_iota(jnp.int32, dims, 0)
    k = lax.broadcasted_iota(jnp.int32, dims, 1)
    n = lax.broadcasted_iota(jnp.int32, dims, 2)
    shift = ((w - n % ZB == k % TS) & (k // TS == n // ZB)).astype(jnp.float32)
    pairs = kernels.reshape(FIELDS, per, TS // 2, 2, TS, TS)
    halves = []
    for e in range(2):
        kt = jnp.transpose(pairs[:, :, :, e], (2, 3, 1, 0, 4)).reshape(TS * TS // 2, TS * nt)
        halves.append(jnp.einsum("rk,wkn->rwn", kt, shift, precision=lax.Precision.HIGHEST))
    rhs = jnp.concatenate(halves, axis=-1)
    return rhs.reshape(TS // 2, 1, TS * (TS + ZB), 2 * nt * ZB)


def im2col_kernel(p_ref, o_ref):
    def body(y, carry):
        for zb in range(o_ref.shape[0]):
            for b in range(TS):
                o_ref[zb, y, :, b * (TS + ZB):(b + 1) * (TS + ZB)] = p_ref[y + b, :, zb * ZB: zb * ZB + TS + ZB]
        return carry
    lax.fori_loop(0, BY, body, 0)


def im2col(padded_t, blocks):
    rows = padded_t.shape[1]
    return pl.pallas_call(
        im2col_kernel,
        out_shape=jax.ShapeDtypeStruct((blocks, BY, rows, TS * (TS + ZB)), jnp.float32),
        in_specs=[pl.BlockSpec(memory_space=pltpu.VMEM)],
        out_specs=pl.BlockSpec(memory_space=pltpu.VMEM),
        cost_estimate=pl.CostEstimate(flops=0, transcendentals=0, bytes_accessed=4 * blocks * BY * rows * TS * (TS + ZB)),
    )(padded_t)


def local(volume, bank, orient, bank_id, counts):
    rows_x = volume.shape[0]
    half = TS // 2
    nt = orient.shape[0]
    grid = volume.reshape(rows_x, BY, BZ)
    len_x = rows_x + TS
    len_y = BY + TS
    len_z = BZ + TS
    blocks = BZ // ZB
    planes = gather_planes(bank, "gx")
    per = nt // FIELDS
    kernels = rotated_kernels(planes, orient, bank_id)
    rhs = toeplitz_rhs(kernels)
    field_in = extended(grid, (("gx", 0),), half)
    padded = jnp.pad(field_in, ((0, 0), (half, TS - half), (half, TS - half)))
    cols = im2col(jnp.transpose(padded[: len_x - 1], (1, 0, 2)), blocks)
    cols = cols.reshape(1, blocks * BY, len_x - 1, TS * (TS + ZB))
    both = lax.conv_general_dilated(
        cols, rhs, (1, 1), "VALID", rhs_dilation=(2, 1),
        dimension_numbers=lax.ConvDimensionNumbers((0, 3, 2, 1), (3, 2, 0, 1), (0, 3, 1, 2)),
        precision=lax.Precision.HIGH,
    )
    numer = both[:, :rows_x, :, : nt * ZB] + both[:, 1:, :, nt * ZB:]
    numer = numer.reshape(rows_x, blocks * BY, nt * ZB)
    pos_x = jnp.arange(len_x, dtype=jnp.int32)
    out_x = jnp.arange(rows_x, dtype=jnp.int32)
    pos_y = half + jnp.arange(BY, dtype=jnp.int32)
    pos_z = half + jnp.arange(BZ, dtype=jnp.int32)
    squares = field_in * field_in
    energy = contract(
        "xyz,zn->xyn", squares, band_table(pos_z, jnp.arange(BZ, dtype=jnp.int32), len_z)
    )
    energy = contract(
        "xyn,ym->xmn", energy, band_table(pos_y, jnp.arange(BY, dtype=jnp.int32), len_y)
    )
    energy = contract("xmn,xl->lmn", energy, band_table(pos_x, out_x, len_x))
    energy = jnp.transpose(energy.reshape(rows_x, BY, blocks, ZB), (0, 2, 1, 3))
    energy = jnp.tile(energy.reshape(rows_x, blocks * BY, ZB), (1, 1, nt))
    scores = numer / jnp.sqrt(energy + epsilon)
    weights = jnp.transpose(counts.astype(jnp.float32).reshape(FIELDS, per)).reshape(nt)
    weighted = jnp.repeat(weights, ZB)[None, None] * jnp.exp(sharpness * scores)
    half_lanes = FIELDS * ZB
    grouped = weighted[:, :, :half_lanes]
    for p in range(1, per):
        grouped = grouped + weighted[:, :, p * half_lanes:(p + 1) * half_lanes]
    totals = weights[:FIELDS]
    for p in range(1, per):
        totals = totals + weights[p * FIELDS:(p + 1) * FIELDS]
    fields = jnp.log(grouped / jnp.repeat(totals, ZB)[None, None])
    fields = fields.reshape(rows_x, blocks, BY, FIELDS, ZB)
    fields = jnp.transpose(fields, (3, 0, 2, 1, 4))
    return fields.reshape(FIELDS, rows_x, BY * BZ)


def solution(mesh):
    in_specs = (P(("grp", "gx"), None), P(None, "gx"), P(), P(), P())
    out_specs = P(None, ("grp", "gx"), None)
    return jax.shard_map(local, mesh=mesh, in_specs=in_specs, out_specs=out_specs, check_vma=False)
```

```python
import jax
import jax.numpy as jnp
import numpy as np
from jax import lax
from jax.experimental import pallas as pl
from jax.experimental.pallas import tpu as pltpu
from jax.sharding import PartitionSpec as P

BY = 8
BZ = 112
TS = 16
NT = 8
FIELDS = 4
ZB = 16

epsilon = 1e-05
sharpness = 80.0
AXIS_ORDERS = np.array([[0, 1, 2], [0, 2, 1], [1, 0, 2], [1, 2, 0], [2, 0, 1], [2, 1, 0]], np.int32)


def extended(x, sides, width):
    for axis, dim in sides:
        size, length = (lax.axis_size(axis), x.shape[dim])
        up = [(i, (i + 1) % size) for i in range(size - 1)]
        down = [(j, i) for i, j in up]
        last = lax.slice_in_dim(x, length - width, length, axis=dim)
        leading = lax.slice_in_dim(x, 0, width, axis=dim)
        before = lax.ppermute(last, axis, up)
        after = lax.ppermute(leading, axis, down)
        x = jnp.concatenate([before, x, after], axis=dim)
    return x


def band_table(positions, targets, period):
    offset = (positions[:, None] - targets[None, :]) % period
    return (offset < TS).astype(jnp.float32)


def contract(letters, data, table):
    return jnp.einsum(letters, data, table, precision=lax.Precision.HIGHEST)


def expand(flag):
    return flag[:, None, None, None]


def gather_planes(bank, axis):
    size = lax.axis_size(axis)
    me = lax.axis_index(axis)
    held = bank[None]
    step = 1
    while step < size:
        radix = min(4, size // step)
        digit = (me // step) % radix
        blocks = [held] + [
            lax.ppermute(held, axis, [(i, i ^ (s * step)) for i in range(size)]) for s in range(1, radix)
        ]
        placed = []
        for d in range(radix):
            value = jnp.zeros_like(held)
            for s in range(radix):
                value = value + jnp.where((digit ^ s) == d, blocks[s], 0.0)
            placed.append(value)
        held = jnp.concatenate(placed, 0)
        step *= radix
    return held


def rotated_kernels(planes, orient, bank_id):
    count = planes.shape[1]
    picked = jnp.zeros((orient.shape[0], TS, TS, TS), jnp.float32)
    for m in range(count):
        base = planes[:, m, :].reshape(TS, TS, TS)
        picked = picked + jnp.where(expand(bank_id == m), base[None], 0.0)
    flips = orient % 8
    for axis_num in range(3):
        bit = (flips // 2**axis_num) % 2 == 1
        picked = jnp.where(expand(bit), jnp.flip(picked, axis=axis_num + 1), picked)
    order_row = orient // 8
    rotated = jnp.zeros_like(picked)
    for row in range(AXIS_ORDERS.shape[0]):
        perm = (0,) + tuple(1 + int(p) for p in np.argsort(AXIS_ORDERS[row]))
        rotated = rotated + jnp.where(expand(order_row == row), jnp.transpose(picked, perm), 0.0)
    flat = rotated.reshape(rotated.shape[0], -1)
    centered = flat - jnp.mean(flat, axis=1, keepdims=True)
    norm = jnp.sqrt(jnp.sum(centered * centered, axis=1, keepdims=True) + epsilon)
    return (centered / norm).reshape(rotated.shape)


def toeplitz_rhs(kernels):
    nt = kernels.shape[0]
    per = nt // FIELDS
    dims = (TS + ZB, 2 * TS * nt, 2 * nt * ZB)
    w = lax.broadcasted_iota(jnp.int32, dims, 0)
    k = lax.broadcasted_iota(jnp.int32, dims, 1)
    n = lax.broadcasted_iota(jnp.int32, dims, 2)
    shift = ((w - n % ZB == k % TS) & (k // TS == n // ZB)).astype(jnp.float32)
    pairs = kernels.reshape(FIELDS, per, TS // 2, 2, TS, TS)
    kt = jnp.transpose(pairs, (2, 4, 3, 1, 0, 5)).reshape(TS * TS // 2, 2 * TS * nt)
    rhs = jnp.einsum("rk,wkn->rwn", kt, shift, precision=lax.Precision.HIGHEST)
    return rhs.reshape(TS // 2, 1, TS * (TS + ZB), 2 * nt * ZB)


def im2col_kernel(p_ref, o_ref):
    def body(y, carry):
        for zb in range(o_ref.shape[0]):
            for b in range(TS):
                o_ref[zb, y, :, b * (TS + ZB):(b + 1) * (TS + ZB)] = p_ref[y + b, :, zb * ZB: zb * ZB + TS + ZB]
        return carry
    lax.fori_loop(0, BY, body, 0)


def im2col(padded_t, blocks):
    rows = padded_t.shape[1]
    return pl.pallas_call(
        im2col_kernel,
        out_shape=jax.ShapeDtypeStruct((blocks, BY, rows, TS * (TS + ZB)), jnp.float32),
        in_specs=[pl.BlockSpec(memory_space=pltpu.VMEM)],
        out_specs=pl.BlockSpec(memory_space=pltpu.VMEM),
        cost_estimate=pl.CostEstimate(flops=0, transcendentals=0, bytes_accessed=4 * blocks * BY * rows * TS * (TS + ZB)),
    )(padded_t)


def local(volume, bank, orient, bank_id, counts):
    rows_x = volume.shape[0]
    half = TS // 2
    nt = orient.shape[0]
    grid = volume.reshape(rows_x, BY, BZ)
    len_x = rows_x + TS
    len_y = BY + TS
    len_z = BZ + TS
    blocks = BZ // ZB
    planes = gather_planes(bank, "gx")
    per = nt // FIELDS
    kernels = rotated_kernels(planes, orient, bank_id)
    rhs = toeplitz_rhs(kernels)
    field_in = extended(grid, (("gx", 0),), half)
    padded = jnp.pad(field_in, ((0, 0), (half, TS - half), (half, TS - half)))
    cols = im2col(jnp.transpose(padded[: len_x - 1], (1, 0, 2)), blocks)
    cols = cols.reshape(1, blocks * BY, len_x - 1, TS * (TS + ZB))
    both = lax.conv_general_dilated(
        cols, rhs, (1, 1), "VALID", rhs_dilation=(2, 1),
        dimension_numbers=lax.ConvDimensionNumbers((0, 3, 2, 1), (3, 2, 0, 1), (0, 3, 1, 2)),
        precision=lax.Precision.HIGH,
    )
    numer = both[:, :rows_x, :, : nt * ZB] + both[:, 1:, :, nt * ZB:]
    numer = numer.reshape(rows_x, blocks * BY, nt * ZB)
    pos_x = jnp.arange(len_x, dtype=jnp.int32)
    out_x = jnp.arange(rows_x, dtype=jnp.int32)
    pos_y = half + jnp.arange(BY, dtype=jnp.int32)
    pos_z = half + jnp.arange(BZ, dtype=jnp.int32)
    squares = field_in * field_in
    energy = contract(
        "xyz,zn->xyn", squares, band_table(pos_z, jnp.arange(BZ, dtype=jnp.int32), len_z)
    )
    energy = contract(
        "xyn,ym->xmn", energy, band_table(pos_y, jnp.arange(BY, dtype=jnp.int32), len_y)
    )
    energy = contract("xmn,xl->lmn", energy, band_table(pos_x, out_x, len_x))
    energy = jnp.transpose(energy.reshape(rows_x, BY, blocks, ZB), (0, 2, 1, 3))
    energy = jnp.tile(energy.reshape(rows_x, blocks * BY, ZB), (1, 1, nt))
    scores = numer / jnp.sqrt(energy + epsilon)
    weights = jnp.transpose(counts.astype(jnp.float32).reshape(FIELDS, per)).reshape(nt)
    weighted = jnp.repeat(weights, ZB)[None, None] * jnp.exp(sharpness * scores)
    half_lanes = FIELDS * ZB
    grouped = weighted[:, :, :half_lanes]
    for p in range(1, per):
        grouped = grouped + weighted[:, :, p * half_lanes:(p + 1) * half_lanes]
    totals = weights[:FIELDS]
    for p in range(1, per):
        totals = totals + weights[p * FIELDS:(p + 1) * FIELDS]
    fields = jnp.log(grouped / jnp.repeat(totals, ZB)[None, None])
    fields = fields.reshape(rows_x, blocks, BY, FIELDS, ZB)
    fields = jnp.transpose(fields, (3, 0, 2, 1, 4))
    return fields.reshape(FIELDS, rows_x, BY * BZ)


def solution(mesh):
    in_specs = (P(("grp", "gx"), None), P(None, "gx"), P(), P(), P())
    out_specs = P(None, ("grp", "gx"), None)
    return jax.shard_map(local, mesh=mesh, in_specs=in_specs, out_specs=out_specs, check_vma=False)
```

```python
import jax
import jax.numpy as jnp
import numpy as np
from jax import lax
from jax.experimental import pallas as pl
from jax.experimental.pallas import tpu as pltpu
from jax.sharding import PartitionSpec as P

BY = 8
BZ = 112
TS = 16
NT = 8
FIELDS = 4
ZB = 16

epsilon = 1e-05
sharpness = 80.0
AXIS_ORDERS = np.array([[0, 1, 2], [0, 2, 1], [1, 0, 2], [1, 2, 0], [2, 0, 1], [2, 1, 0]], np.int32)


def extended(x, sides, width):
    for axis, dim in sides:
        size, length = (lax.axis_size(axis), x.shape[dim])
        up = [(i, (i + 1) % size) for i in range(size - 1)]
        down = [(j, i) for i, j in up]
        last = lax.slice_in_dim(x, length - width, length, axis=dim)
        leading = lax.slice_in_dim(x, 0, width, axis=dim)
        before = lax.ppermute(last, axis, up)
        after = lax.ppermute(leading, axis, down)
        x = jnp.concatenate([before, x, after], axis=dim)
    return x


def band_table(positions, targets, period):
    offset = (positions[:, None] - targets[None, :]) % period
    return (offset < TS).astype(jnp.float32)


def contract(letters, data, table):
    return jnp.einsum(letters, data, table, precision=lax.Precision.HIGHEST)


def expand(flag):
    return flag[:, None, None, None]


def gather_planes(bank, axis):
    size = lax.axis_size(axis)
    me = lax.axis_index(axis)
    held = bank[None]
    step = 1
    while step < size:
        radix = min(4, size // step)
        digit = (me // step) % radix
        blocks = [held] + [
            lax.ppermute(held, axis, [(i, i ^ (s * step)) for i in range(size)]) for s in range(1, radix)
        ]
        placed = []
        for d in range(radix):
            value = jnp.zeros_like(held)
            for s in range(radix):
                value = value + jnp.where((digit ^ s) == d, blocks[s], 0.0)
            placed.append(value)
        held = jnp.concatenate(placed, 0)
        step *= radix
    return held


def rotated_kernels(planes, orient, bank_id):
    count = planes.shape[1]
    picked = jnp.zeros((orient.shape[0], TS, TS, TS), jnp.float32)
    for m in range(count):
        base = planes[:, m, :].reshape(TS, TS, TS)
        picked = picked + jnp.where(expand(bank_id == m), base[None], 0.0)
    flips = orient % 8
    for axis_num in range(3):
        bit = (flips // 2**axis_num) % 2 == 1
        picked = jnp.where(expand(bit), jnp.flip(picked, axis=axis_num + 1), picked)
    order_row = orient // 8
    rotated = jnp.zeros_like(picked)
    for row in range(AXIS_ORDERS.shape[0]):
        perm = (0,) + tuple(1 + int(p) for p in np.argsort(AXIS_ORDERS[row]))
        rotated = rotated + jnp.where(expand(order_row == row), jnp.transpose(picked, perm), 0.0)
    flat = rotated.reshape(rotated.shape[0], -1)
    centered = flat - jnp.mean(flat, axis=1, keepdims=True)
    norm = jnp.sqrt(jnp.sum(centered * centered, axis=1, keepdims=True) + epsilon)
    return (centered / norm).reshape(rotated.shape)


def toeplitz_rhs(kernels):
    nt = kernels.shape[0]
    per = nt // FIELDS
    dims = (TS + ZB, 2 * TS * nt, 2 * nt * ZB)
    w = lax.broadcasted_iota(jnp.int32, dims, 0)
    k = lax.broadcasted_iota(jnp.int32, dims, 1)
    n = lax.broadcasted_iota(jnp.int32, dims, 2)
    shift = ((w - n % ZB == k % TS) & (k // TS == n // ZB)).astype(jnp.float32)
    pairs = kernels.reshape(FIELDS, per, TS // 2, 2, TS, TS)
    kt = jnp.transpose(pairs, (2, 4, 3, 1, 0, 5)).reshape(TS * TS // 2, 2 * TS * nt)
    rhs = jnp.einsum("rk,wkn->rwn", kt, shift, precision=lax.Precision.HIGHEST)
    return rhs.reshape(TS // 2, 1, TS * (TS + ZB), 2 * nt * ZB)


def im2col_kernel(p_ref, o_ref):
    def body(y, carry):
        for zb in range(o_ref.shape[0]):
            for b in range(TS):
                o_ref[zb, y, :, b * (TS + ZB):(b + 1) * (TS + ZB)] = p_ref[y + b, :, zb * ZB: zb * ZB + TS + ZB]
        return carry
    lax.fori_loop(0, BY, body, 0)


def im2col(padded_t, blocks):
    rows = padded_t.shape[1]
    return pl.pallas_call(
        im2col_kernel,
        out_shape=jax.ShapeDtypeStruct((blocks, BY, rows, TS * (TS + ZB)), jnp.float32),
        in_specs=[pl.BlockSpec(memory_space=pltpu.VMEM)],
        out_specs=pl.BlockSpec(memory_space=pltpu.VMEM),
        cost_estimate=pl.CostEstimate(flops=0, transcendentals=0, bytes_accessed=4 * blocks * BY * rows * TS * (TS + ZB)),
    )(padded_t)


def post_kernel(both_ref, energy_ref, wl_ref, tl_ref, o_ref):
    rows = o_ref.shape[1]
    lanes = wl_ref.shape[-1]
    half_lanes = tl_ref.shape[-1]
    numer = both_ref[:, 0:rows, 0:lanes] + both_ref[:, 1:rows + 1, lanes:2 * lanes]
    scores = numer / jnp.sqrt(energy_ref[...] + epsilon)
    weighted = wl_ref[...] * jnp.exp(sharpness * scores)
    grouped = weighted[:, :, 0:half_lanes]
    for p in range(1, lanes // half_lanes):
        grouped = grouped + weighted[:, :, p * half_lanes:(p + 1) * half_lanes]
    fields = jnp.log(grouped / tl_ref[...])
    blocks = both_ref.shape[0] // BY
    for k in range(o_ref.shape[0]):
        for zb in range(blocks):
            for y in range(BY):
                at = y * BZ + zb * ZB
                o_ref[k, :, at:at + ZB] = fields[zb * BY + y, :, k * ZB:(k + 1) * ZB]


def post(both, energy, wl, tl, rows_x):
    return pl.pallas_call(
        post_kernel,
        out_shape=jax.ShapeDtypeStruct((FIELDS, rows_x, BY * BZ), jnp.float32),
        in_specs=[pl.BlockSpec(memory_space=pltpu.VMEM)] * 4,
        out_specs=pl.BlockSpec(memory_space=pltpu.VMEM),
    )(both, energy, wl, tl)


def local(volume, bank, orient, bank_id, counts):
    rows_x = volume.shape[0]
    half = TS // 2
    nt = orient.shape[0]
    grid = volume.reshape(rows_x, BY, BZ)
    len_x = rows_x + TS
    len_y = BY + TS
    len_z = BZ + TS
    blocks = BZ // ZB
    planes = gather_planes(bank, "gx")
    per = nt // FIELDS
    kernels = rotated_kernels(planes, orient, bank_id)
    rhs = toeplitz_rhs(kernels)
    field_in = extended(grid, (("gx", 0),), half)
    padded = jnp.pad(field_in, ((0, 0), (half, TS - half), (half, TS - half)))
    cols = im2col(jnp.transpose(padded[: len_x - 1], (1, 0, 2)), blocks)
    cols = cols.reshape(1, blocks * BY, len_x - 1, TS * (TS + ZB))
    both = lax.conv_general_dilated(
        cols, rhs, (1, 1), "VALID", rhs_dilation=(2, 1),
        dimension_numbers=lax.ConvDimensionNumbers((0, 3, 2, 1), (3, 2, 0, 1), (0, 3, 2, 1)),
        precision=lax.Precision.HIGH,
    )
    pos_x = jnp.arange(len_x, dtype=jnp.int32)
    out_x = jnp.arange(rows_x, dtype=jnp.int32)
    pos_y = half + jnp.arange(BY, dtype=jnp.int32)
    pos_z = half + jnp.arange(BZ, dtype=jnp.int32)
    squares = field_in * field_in
    energy = contract(
        "xyz,zn->xyn", squares, band_table(pos_z, jnp.arange(BZ, dtype=jnp.int32), len_z)
    )
    energy = contract(
        "xyn,ym->xmn", energy, band_table(pos_y, jnp.arange(BY, dtype=jnp.int32), len_y)
    )
    energy = contract("xmn,xl->lmn", energy, band_table(pos_x, out_x, len_x))
    energy = jnp.transpose(energy.reshape(rows_x, BY, blocks, ZB), (2, 1, 0, 3))
    energy = jnp.tile(energy.reshape(blocks * BY, rows_x, ZB), (1, 1, nt))
    weights = jnp.transpose(counts.astype(jnp.float32).reshape(FIELDS, per)).reshape(nt)
    totals = weights[:FIELDS]
    for p in range(1, per):
        totals = totals + weights[p * FIELDS:(p + 1) * FIELDS]
    wl = jnp.repeat(weights, ZB)[None, None]
    tl = jnp.repeat(totals, ZB)[None, None]
    return post(both[0], energy, wl, tl, rows_x)


def solution(mesh):
    in_specs = (P(("grp", "gx"), None), P(None, "gx"), P(), P(), P())
    out_specs = P(None, ("grp", "gx"), None)
    return jax.shard_map(local, mesh=mesh, in_specs=in_specs, out_specs=out_specs, check_vma=False)
```

```python
import jax
import jax.numpy as jnp
import numpy as np
from jax import lax
from jax.experimental import pallas as pl
from jax.experimental.pallas import tpu as pltpu
from jax.sharding import PartitionSpec as P

BY = 8
BZ = 112
TS = 16
NT = 8
FIELDS = 4
ZB = 16

epsilon = 1e-05
sharpness = 80.0
AXIS_ORDERS = np.array([[0, 1, 2], [0, 2, 1], [1, 0, 2], [1, 2, 0], [2, 0, 1], [2, 1, 0]], np.int32)


def extended(x, sides, width):
    for axis, dim in sides:
        size, length = (lax.axis_size(axis), x.shape[dim])
        up = [(i, (i + 1) % size) for i in range(size - 1)]
        down = [(j, i) for i, j in up]
        last = lax.slice_in_dim(x, length - width, length, axis=dim)
        leading = lax.slice_in_dim(x, 0, width, axis=dim)
        before = lax.ppermute(last, axis, up)
        after = lax.ppermute(leading, axis, down)
        x = jnp.concatenate([before, x, after], axis=dim)
    return x


def band_table(positions, targets, period):
    offset = (positions[:, None] - targets[None, :]) % period
    return (offset < TS).astype(jnp.float32)


def contract(letters, data, table):
    return jnp.einsum(letters, data, table, precision=lax.Precision.HIGHEST)


def expand(flag):
    return flag[:, None, None, None]


def gather_planes(bank, axis):
    size = lax.axis_size(axis)
    me = lax.axis_index(axis)
    held = bank[None]
    step = 1
    while step < size:
        radix = min(4, size // step)
        digit = (me // step) % radix
        blocks = [held] + [
            lax.ppermute(held, axis, [(i, i ^ (s * step)) for i in range(size)]) for s in range(1, radix)
        ]
        placed = []
        for d in range(radix):
            value = jnp.zeros_like(held)
            for s in range(radix):
                value = value + jnp.where((digit ^ s) == d, blocks[s], 0.0)
            placed.append(value)
        held = jnp.concatenate(placed, 0)
        step *= radix
    return held


def rotated_kernels(planes, orient, bank_id):
    count = planes.shape[1]
    picked = jnp.zeros((orient.shape[0], TS, TS, TS), jnp.float32)
    for m in range(count):
        base = planes[:, m, :].reshape(TS, TS, TS)
        picked = picked + jnp.where(expand(bank_id == m), base[None], 0.0)
    flips = orient % 8
    for axis_num in range(3):
        bit = (flips // 2**axis_num) % 2 == 1
        picked = jnp.where(expand(bit), jnp.flip(picked, axis=axis_num + 1), picked)
    order_row = orient // 8
    rotated = jnp.zeros_like(picked)
    for row in range(AXIS_ORDERS.shape[0]):
        perm = (0,) + tuple(1 + int(p) for p in np.argsort(AXIS_ORDERS[row]))
        rotated = rotated + jnp.where(expand(order_row == row), jnp.transpose(picked, perm), 0.0)
    flat = rotated.reshape(rotated.shape[0], -1)
    centered = flat - jnp.mean(flat, axis=1, keepdims=True)
    norm = jnp.sqrt(jnp.sum(centered * centered, axis=1, keepdims=True) + epsilon)
    return (centered / norm).reshape(rotated.shape)


def toeplitz_rhs(kernels):
    nt = kernels.shape[0]
    per = nt // FIELDS
    dims = (TS + ZB, 2 * TS * nt, 2 * nt * ZB)
    w = lax.broadcasted_iota(jnp.int32, dims, 0)
    k = lax.broadcasted_iota(jnp.int32, dims, 1)
    n = lax.broadcasted_iota(jnp.int32, dims, 2)
    shift = ((w - n % ZB == k % TS) & (k // TS == n // ZB)).astype(jnp.float32)
    pairs = kernels.reshape(FIELDS, per, TS // 2, 2, TS, TS)
    kt = jnp.transpose(pairs, (2, 4, 3, 1, 0, 5)).reshape(TS * TS // 2, 2 * TS * nt)
    rhs = jnp.einsum("rk,wkn->rwn", kt, shift, precision=lax.Precision.HIGHEST)
    return rhs.reshape(TS // 2, 1, TS * (TS + ZB), 2 * nt * ZB)


def im2col_kernel(p_ref, o_ref):
    def body(y, carry):
        for zb in range(o_ref.shape[0]):
            for b in range(TS):
                o_ref[zb, y, :, b * (TS + ZB):(b + 1) * (TS + ZB)] = p_ref[y + b, :, zb * ZB: zb * ZB + TS + ZB]
        return carry
    lax.fori_loop(0, BY, body, 0)


def im2col(padded_t, blocks):
    rows = padded_t.shape[1]
    return pl.pallas_call(
        im2col_kernel,
        out_shape=jax.ShapeDtypeStruct((blocks, BY, rows, TS * (TS + ZB)), jnp.float32),
        in_specs=[pl.BlockSpec(memory_space=pltpu.VMEM)],
        out_specs=pl.BlockSpec(memory_space=pltpu.VMEM),
        cost_estimate=pl.CostEstimate(flops=0, transcendentals=0, bytes_accessed=4 * blocks * BY * rows * TS * (TS + ZB)),
    )(padded_t)


def post_kernel(both_ref, energy_ref, wl_ref, tl_ref, o_ref, fields_ref):
    rows = o_ref.shape[1]
    lanes = wl_ref.shape[-1]
    half_lanes = tl_ref.shape[-1]
    numer = both_ref[0:rows, :, 0:lanes] + both_ref[1:rows + 1, :, lanes:2 * lanes]
    scores = numer / jnp.sqrt(energy_ref[...] + epsilon)
    weighted = wl_ref[...] * jnp.exp(sharpness * scores)
    grouped = weighted[:, :, 0:half_lanes]
    for p in range(1, lanes // half_lanes):
        grouped = grouped + weighted[:, :, p * half_lanes:(p + 1) * half_lanes]
    fields_ref[...] = jnp.log(grouped / tl_ref[...])
    blocks = both_ref.shape[1] // BY
    for k in range(o_ref.shape[0]):
        for zb in range(blocks):
            for y in range(BY):
                at = y * BZ + zb * ZB
                o_ref[k, :, at:at + ZB] = fields_ref[:, zb * BY + y, k * ZB:(k + 1) * ZB]


def post(both, energy, wl, tl, rows_x):
    return pl.pallas_call(
        post_kernel,
        out_shape=jax.ShapeDtypeStruct((FIELDS, rows_x, BY * BZ), jnp.float32),
        in_specs=[pl.BlockSpec(memory_space=pltpu.VMEM)] * 4,
        out_specs=pl.BlockSpec(memory_space=pltpu.VMEM),
        scratch_shapes=[pltpu.VMEM((rows_x, both.shape[1], tl.shape[-1]), jnp.float32)],
    )(both, energy, wl, tl)


def local(volume, bank, orient, bank_id, counts):
    rows_x = volume.shape[0]
    half = TS // 2
    nt = orient.shape[0]
    grid = volume.reshape(rows_x, BY, BZ)
    len_x = rows_x + TS
    len_y = BY + TS
    len_z = BZ + TS
    blocks = BZ // ZB
    planes = gather_planes(bank, "gx")
    per = nt // FIELDS
    kernels = rotated_kernels(planes, orient, bank_id)
    rhs = toeplitz_rhs(kernels)
    field_in = extended(grid, (("gx", 0),), half)
    padded = jnp.pad(field_in, ((0, 0), (half, TS - half), (half, TS - half)))
    cols = im2col(jnp.transpose(padded[: len_x - 1], (1, 0, 2)), blocks)
    cols = cols.reshape(1, blocks * BY, len_x - 1, TS * (TS + ZB))
    both = lax.conv_general_dilated(
        cols, rhs, (1, 1), "VALID", rhs_dilation=(2, 1),
        dimension_numbers=lax.ConvDimensionNumbers((0, 3, 2, 1), (3, 2, 0, 1), (0, 3, 1, 2)),
        precision=lax.Precision.HIGH,
    )
    pos_x = jnp.arange(len_x, dtype=jnp.int32)
    out_x = jnp.arange(rows_x, dtype=jnp.int32)
    pos_y = half + jnp.arange(BY, dtype=jnp.int32)
    pos_z = half + jnp.arange(BZ, dtype=jnp.int32)
    squares = field_in * field_in
    energy = contract(
        "xyz,zn->xyn", squares, band_table(pos_z, jnp.arange(BZ, dtype=jnp.int32), len_z)
    )
    energy = contract(
        "xyn,ym->xmn", energy, band_table(pos_y, jnp.arange(BY, dtype=jnp.int32), len_y)
    )
    energy = contract("xmn,xl->lmn", energy, band_table(pos_x, out_x, len_x))
    energy = jnp.transpose(energy.reshape(rows_x, BY, blocks, ZB), (0, 2, 1, 3))
    energy = jnp.tile(energy.reshape(rows_x, blocks * BY, ZB), (1, 1, nt))
    weights = jnp.transpose(counts.astype(jnp.float32).reshape(FIELDS, per)).reshape(nt)
    totals = weights[:FIELDS]
    for p in range(1, per):
        totals = totals + weights[p * FIELDS:(p + 1) * FIELDS]
    wl = jnp.repeat(weights, ZB)[None, None]
    tl = jnp.repeat(totals, ZB)[None, None]
    return post(both[0], energy, wl, tl, rows_x)


def solution(mesh):
    in_specs = (P(("grp", "gx"), None), P(None, "gx"), P(), P(), P())
    out_specs = P(None, ("grp", "gx"), None)
    return jax.shard_map(local, mesh=mesh, in_specs=in_specs, out_specs=out_specs, check_vma=False)
```

```python
import jax
import jax.numpy as jnp
import numpy as np
from jax import lax
from jax.experimental import pallas as pl
from jax.experimental.pallas import tpu as pltpu
from jax.sharding import PartitionSpec as P

BY = 8
BZ = 112
TS = 16
NT = 8
FIELDS = 4
ZB = 16

epsilon = 1e-05
sharpness = 80.0
AXIS_ORDERS = np.array([[0, 1, 2], [0, 2, 1], [1, 0, 2], [1, 2, 0], [2, 0, 1], [2, 1, 0]], np.int32)


def extended(x, sides, width):
    for axis, dim in sides:
        size, length = (lax.axis_size(axis), x.shape[dim])
        up = [(i, (i + 1) % size) for i in range(size - 1)]
        down = [(j, i) for i, j in up]
        last = lax.slice_in_dim(x, length - width, length, axis=dim)
        leading = lax.slice_in_dim(x, 0, width, axis=dim)
        before = lax.ppermute(last, axis, up)
        after = lax.ppermute(leading, axis, down)
        x = jnp.concatenate([before, x, after], axis=dim)
    return x


def band_table(positions, targets, period):
    offset = (positions[:, None] - targets[None, :]) % period
    return (offset < TS).astype(jnp.float32)


def contract(letters, data, table):
    return jnp.einsum(letters, data, table, precision=lax.Precision.HIGHEST)


def expand(flag):
    return flag[:, None, None, None]


def gather_planes(bank, axis):
    size = lax.axis_size(axis)
    me = lax.axis_index(axis)
    held = bank[None]
    step = 1
    while step < size:
        radix = min(4, size // step)
        digit = (me // step) % radix
        blocks = [held] + [
            lax.ppermute(held, axis, [(i, i ^ (s * step)) for i in range(size)]) for s in range(1, radix)
        ]
        placed = []
        for d in range(radix):
            value = jnp.zeros_like(held)
            for s in range(radix):
                value = value + jnp.where((digit ^ s) == d, blocks[s], 0.0)
            placed.append(value)
        held = jnp.concatenate(placed, 0)
        step *= radix
    return held


def rotated_kernels(planes, orient, bank_id):
    count = planes.shape[1]
    picked = jnp.zeros((orient.shape[0], TS, TS, TS), jnp.float32)
    for m in range(count):
        base = planes[:, m, :].reshape(TS, TS, TS)
        picked = picked + jnp.where(expand(bank_id == m), base[None], 0.0)
    flips = orient % 8
    for axis_num in range(3):
        bit = (flips // 2**axis_num) % 2 == 1
        picked = jnp.where(expand(bit), jnp.flip(picked, axis=axis_num + 1), picked)
    order_row = orient // 8
    rotated = jnp.zeros_like(picked)
    for row in range(AXIS_ORDERS.shape[0]):
        perm = (0,) + tuple(1 + int(p) for p in np.argsort(AXIS_ORDERS[row]))
        rotated = rotated + jnp.where(expand(order_row == row), jnp.transpose(picked, perm), 0.0)
    flat = rotated.reshape(rotated.shape[0], -1)
    centered = flat - jnp.mean(flat, axis=1, keepdims=True)
    norm = jnp.sqrt(jnp.sum(centered * centered, axis=1, keepdims=True) + epsilon)
    return (centered / norm).reshape(rotated.shape)


def toeplitz_rhs(kernels):
    nt = kernels.shape[0]
    per = nt // FIELDS
    dims = (TS + ZB, 2 * TS * nt, 2 * nt * ZB)
    w = lax.broadcasted_iota(jnp.int32, dims, 0)
    k = lax.broadcasted_iota(jnp.int32, dims, 1)
    n = lax.broadcasted_iota(jnp.int32, dims, 2)
    shift = ((w - n % ZB == k % TS) & (k // TS == n // ZB)).astype(jnp.float32)
    pairs = kernels.reshape(FIELDS, per, TS // 2, 2, TS, TS)
    kt = jnp.transpose(pairs, (2, 4, 3, 1, 0, 5)).reshape(TS * TS // 2, 2 * TS * nt)
    rhs = jnp.einsum("rk,wkn->rwn", kt, shift, precision=lax.Precision.HIGHEST)
    return rhs.reshape(TS // 2, 1, TS * (TS + ZB), 2 * nt * ZB)


def im2col_kernel(p_ref, o_ref):
    def body(y, carry):
        for zb in range(o_ref.shape[0]):
            for b in range(TS):
                o_ref[zb, y, :, b * (TS + ZB):(b + 1) * (TS + ZB)] = p_ref[y + b, :, zb * ZB: zb * ZB + TS + ZB]
        return carry
    lax.fori_loop(0, BY, body, 0)


def im2col(padded_t, blocks):
    rows = padded_t.shape[1]
    return pl.pallas_call(
        im2col_kernel,
        out_shape=jax.ShapeDtypeStruct((blocks, BY, rows, TS * (TS + ZB)), jnp.float32),
        in_specs=[pl.BlockSpec(memory_space=pltpu.VMEM)],
        out_specs=pl.BlockSpec(memory_space=pltpu.VMEM),
        cost_estimate=pl.CostEstimate(flops=0, transcendentals=0, bytes_accessed=4 * blocks * BY * rows * TS * (TS + ZB)),
    )(padded_t)


def post_kernel(both_ref, energy_ref, wl_ref, tl_ref, o_ref, fields_ref):
    rows = o_ref.shape[1]
    lanes = wl_ref.shape[-1]
    half_lanes = tl_ref.shape[-1]
    numer = both_ref[0:rows, :, :, 0:lanes] + both_ref[1:rows + 1, :, :, lanes:2 * lanes]
    scores = numer / jnp.sqrt(energy_ref[...] + epsilon)
    weighted = wl_ref[...] * jnp.exp(sharpness * scores)
    grouped = weighted[..., 0:half_lanes]
    for p in range(1, lanes // half_lanes):
        grouped = grouped + weighted[..., p * half_lanes:(p + 1) * half_lanes]
    fields_ref[...] = jnp.log(grouped / tl_ref[...])
    blocks = both_ref.shape[2]
    for k in range(o_ref.shape[0]):
        for zb in range(blocks):
            for y in range(BY):
                at = y * BZ + zb * ZB
                o_ref[k, :, at:at + ZB] = fields_ref[:, y, zb, k * ZB:(k + 1) * ZB]


def post(both, energy, wl, tl, rows_x):
    return pl.pallas_call(
        post_kernel,
        out_shape=jax.ShapeDtypeStruct((FIELDS, rows_x, BY * BZ), jnp.float32),
        in_specs=[pl.BlockSpec(memory_space=pltpu.VMEM)] * 4,
        out_specs=pl.BlockSpec(memory_space=pltpu.VMEM),
        scratch_shapes=[pltpu.VMEM((rows_x, both.shape[1], both.shape[2], tl.shape[-1]), jnp.float32)],
    )(both, energy, wl, tl)


def local(volume, bank, orient, bank_id, counts):
    rows_x = volume.shape[0]
    half = TS // 2
    nt = orient.shape[0]
    grid = volume.reshape(rows_x, BY, BZ)
    len_x = rows_x + TS
    len_y = BY + TS
    len_z = BZ + TS
    blocks = BZ // ZB
    planes = gather_planes(bank, "gx")
    per = nt // FIELDS
    kernels = rotated_kernels(planes, orient, bank_id)
    rhs = toeplitz_rhs(kernels)
    field_in = extended(grid, (("gx", 0),), half)
    padded = jnp.pad(field_in, ((0, 0), (half, TS - half), (half, TS - half)))
    cols = im2col(jnp.transpose(padded[: len_x - 1], (1, 0, 2)), blocks)

    both = lax.conv_general_dilated(
        cols, rhs, (1, 1), "VALID", rhs_dilation=(2, 1),
        dimension_numbers=lax.ConvDimensionNumbers((0, 3, 2, 1), (3, 2, 0, 1), (2, 3, 0, 1)),
        precision=lax.Precision.HIGH,
    )
    pos_x = jnp.arange(len_x, dtype=jnp.int32)
    out_x = jnp.arange(rows_x, dtype=jnp.int32)
    pos_y = half + jnp.arange(BY, dtype=jnp.int32)
    pos_z = half + jnp.arange(BZ, dtype=jnp.int32)
    squares = field_in * field_in
    energy = contract(
        "xyz,zn->xyn", squares, band_table(pos_z, jnp.arange(BZ, dtype=jnp.int32), len_z)
    )
    energy = contract(
        "xyn,ym->xmn", energy, band_table(pos_y, jnp.arange(BY, dtype=jnp.int32), len_y)
    )
    energy = contract("xmn,xl->lmn", energy, band_table(pos_x, out_x, len_x))
    energy = jnp.tile(energy.reshape(rows_x, BY, blocks, ZB), (1, 1, 1, nt))
    weights = jnp.transpose(counts.astype(jnp.float32).reshape(FIELDS, per)).reshape(nt)
    totals = weights[:FIELDS]
    for p in range(1, per):
        totals = totals + weights[p * FIELDS:(p + 1) * FIELDS]
    wl = jnp.repeat(weights, ZB)[None, None, None]
    tl = jnp.repeat(totals, ZB)[None, None, None]
    return post(both, energy, wl, tl, rows_x)


def solution(mesh):
    in_specs = (P(("grp", "gx"), None), P(None, "gx"), P(), P(), P())
    out_specs = P(None, ("grp", "gx"), None)
    return jax.shard_map(local, mesh=mesh, in_specs=in_specs, out_specs=out_specs, check_vma=False)
```

```python
import jax
import jax.numpy as jnp
import numpy as np
from jax import lax
from jax.experimental import pallas as pl
from jax.experimental.pallas import tpu as pltpu
from jax.sharding import PartitionSpec as P

BY = 8
BZ = 112
TS = 16
NT = 8
FIELDS = 4
ZB = 16

epsilon = 1e-05
sharpness = 80.0
AXIS_ORDERS = np.array([[0, 1, 2], [0, 2, 1], [1, 0, 2], [1, 2, 0], [2, 0, 1], [2, 1, 0]], np.int32)


def extended(x, sides, width):
    for axis, dim in sides:
        size, length = (lax.axis_size(axis), x.shape[dim])
        up = [(i, (i + 1) % size) for i in range(size - 1)]
        down = [(j, i) for i, j in up]
        last = lax.slice_in_dim(x, length - width, length, axis=dim)
        leading = lax.slice_in_dim(x, 0, width, axis=dim)
        before = lax.ppermute(last, axis, up)
        after = lax.ppermute(leading, axis, down)
        x = jnp.concatenate([before, x, after], axis=dim)
    return x


def band_table(positions, targets, period):
    offset = (positions[:, None] - targets[None, :]) % period
    return (offset < TS).astype(jnp.float32)


def contract(letters, data, table):
    return jnp.einsum(letters, data, table, precision=lax.Precision.HIGHEST)


def expand(flag):
    return flag[:, None, None, None]


def gather_planes(bank, axis):
    size = lax.axis_size(axis)
    me = lax.axis_index(axis)
    held = bank[None]
    step = 1
    while step < size:
        radix = min(4, size // step)
        digit = (me // step) % radix
        blocks = [held] + [
            lax.ppermute(held, axis, [(i, i ^ (s * step)) for i in range(size)]) for s in range(1, radix)
        ]
        placed = []
        for d in range(radix):
            value = jnp.zeros_like(held)
            for s in range(radix):
                value = value + jnp.where((digit ^ s) == d, blocks[s], 0.0)
            placed.append(value)
        held = jnp.concatenate(placed, 0)
        step *= radix
    return held


def rotated_kernels(planes, orient, bank_id):
    count = planes.shape[1]
    picked = jnp.zeros((orient.shape[0], TS, TS, TS), jnp.float32)
    for m in range(count):
        base = planes[:, m, :].reshape(TS, TS, TS)
        picked = picked + jnp.where(expand(bank_id == m), base[None], 0.0)
    flips = orient % 8
    for axis_num in range(3):
        bit = (flips // 2**axis_num) % 2 == 1
        picked = jnp.where(expand(bit), jnp.flip(picked, axis=axis_num + 1), picked)
    order_row = orient // 8
    rotated = jnp.zeros_like(picked)
    for row in range(AXIS_ORDERS.shape[0]):
        perm = (0,) + tuple(1 + int(p) for p in np.argsort(AXIS_ORDERS[row]))
        rotated = rotated + jnp.where(expand(order_row == row), jnp.transpose(picked, perm), 0.0)
    flat = rotated.reshape(rotated.shape[0], -1)
    centered = flat - jnp.mean(flat, axis=1, keepdims=True)
    norm = jnp.sqrt(jnp.sum(centered * centered, axis=1, keepdims=True) + epsilon)
    return (centered / norm).reshape(rotated.shape)


def toeplitz_rhs(kernels):
    nt = kernels.shape[0]
    per = nt // FIELDS
    dims = (TS + ZB, 2 * TS * nt, 2 * nt * ZB)
    w = lax.broadcasted_iota(jnp.int32, dims, 0)
    k = lax.broadcasted_iota(jnp.int32, dims, 1)
    n = lax.broadcasted_iota(jnp.int32, dims, 2)
    shift = ((w - n % ZB == k % TS) & (k // TS == n // ZB)).astype(jnp.float32)
    pairs = kernels.reshape(FIELDS, per, TS // 2, 2, TS, TS)
    kt = jnp.transpose(pairs, (2, 4, 3, 1, 0, 5)).reshape(TS * TS // 2, 2 * TS * nt)
    rhs = jnp.einsum("rk,wkn->rwn", kt, shift, precision=lax.Precision.HIGHEST)
    return rhs.reshape(TS // 2, 1, TS * (TS + ZB), 2 * nt * ZB)


def im2col_kernel(p_ref, o_ref):
    def body(y, carry):
        for zb in range(o_ref.shape[0]):
            for b in range(TS):
                o_ref[zb, y, :, b * (TS + ZB):(b + 1) * (TS + ZB)] = p_ref[y + b, :, zb * ZB: zb * ZB + TS + ZB]
        return carry
    lax.fori_loop(0, BY, body, 0)


def im2col(padded_t, blocks):
    rows = padded_t.shape[1]
    return pl.pallas_call(
        im2col_kernel,
        out_shape=jax.ShapeDtypeStruct((blocks, BY, rows, TS * (TS + ZB)), jnp.float32),
        in_specs=[pl.BlockSpec(memory_space=pltpu.VMEM)],
        out_specs=pl.BlockSpec(memory_space=pltpu.VMEM),
        cost_estimate=pl.CostEstimate(flops=0, transcendentals=0, bytes_accessed=4 * blocks * BY * rows * TS * (TS + ZB)),
    )(padded_t)


def post_kernel(both_ref, energy_ref, wl_ref, tl_ref, o_ref, fields_ref):
    rows = o_ref.shape[1]
    lanes = wl_ref.shape[-1]
    half_lanes = tl_ref.shape[-1]
    numer = both_ref[0:rows, :, :, 0:lanes] + both_ref[1:rows + 1, :, :, lanes:2 * lanes]
    numer = numer.reshape(rows, -1, lanes)
    scores = numer / jnp.sqrt(energy_ref[...] + epsilon)
    weighted = wl_ref[...] * jnp.exp(sharpness * scores)
    grouped = weighted[:, :, 0:half_lanes]
    for p in range(1, lanes // half_lanes):
        grouped = grouped + weighted[:, :, p * half_lanes:(p + 1) * half_lanes]
    fields_ref[...] = jnp.log(grouped / tl_ref[...])
    blocks = both_ref.shape[1]
    for k in range(o_ref.shape[0]):
        for zb in range(blocks):
            for y in range(BY):
                at = y * BZ + zb * ZB
                o_ref[k, :, at:at + ZB] = fields_ref[:, zb * BY + y, k * ZB:(k + 1) * ZB]


def post(both, energy, wl, tl, rows_x):
    return pl.pallas_call(
        post_kernel,
        out_shape=jax.ShapeDtypeStruct((FIELDS, rows_x, BY * BZ), jnp.float32),
        in_specs=[pl.BlockSpec(memory_space=pltpu.VMEM)] * 4,
        out_specs=pl.BlockSpec(memory_space=pltpu.VMEM),
        scratch_shapes=[pltpu.VMEM((rows_x, both.shape[1] * both.shape[2], tl.shape[-1]), jnp.float32)],
    )(both, energy, wl, tl)


def local(volume, bank, orient, bank_id, counts):
    rows_x = volume.shape[0]
    half = TS // 2
    nt = orient.shape[0]
    grid = volume.reshape(rows_x, BY, BZ)
    len_x = rows_x + TS
    len_y = BY + TS
    len_z = BZ + TS
    blocks = BZ // ZB
    planes = gather_planes(bank, "gx")
    per = nt // FIELDS
    kernels = rotated_kernels(planes, orient, bank_id)
    rhs = toeplitz_rhs(kernels)
    field_in = extended(grid, (("gx", 0),), half)
    padded = jnp.pad(field_in, ((0, 0), (half, TS - half), (half, TS - half)))
    cols = im2col(jnp.transpose(padded[: len_x - 1], (1, 0, 2)), blocks)

    both = lax.conv_general_dilated(
        cols, rhs, (1, 1), "VALID", rhs_dilation=(2, 1),
        dimension_numbers=lax.ConvDimensionNumbers((0, 3, 2, 1), (3, 2, 0, 1), (1, 3, 0, 2)),
        precision=lax.Precision.HIGH,
    )
    pos_x = jnp.arange(len_x, dtype=jnp.int32)
    out_x = jnp.arange(rows_x, dtype=jnp.int32)
    pos_y = half + jnp.arange(BY, dtype=jnp.int32)
    pos_z = half + jnp.arange(BZ, dtype=jnp.int32)
    squares = field_in * field_in
    energy = contract(
        "xyz,zn->xyn", squares, band_table(pos_z, jnp.arange(BZ, dtype=jnp.int32), len_z)
    )
    energy = contract(
        "xyn,ym->xmn", energy, band_table(pos_y, jnp.arange(BY, dtype=jnp.int32), len_y)
    )
    energy = contract("xmn,xl->lmn", energy, band_table(pos_x, out_x, len_x))
    energy = jnp.transpose(energy.reshape(rows_x, BY, blocks, ZB), (0, 2, 1, 3))
    energy = jnp.tile(energy.reshape(rows_x, blocks * BY, ZB), (1, 1, nt))
    weights = jnp.transpose(counts.astype(jnp.float32).reshape(FIELDS, per)).reshape(nt)
    totals = weights[:FIELDS]
    for p in range(1, per):
        totals = totals + weights[p * FIELDS:(p + 1) * FIELDS]
    wl = jnp.repeat(weights, ZB)[None, None]
    tl = jnp.repeat(totals, ZB)[None, None]
    return post(both, energy, wl, tl, rows_x)


def solution(mesh):
    in_specs = (P(("grp", "gx"), None), P(None, "gx"), P(), P(), P())
    out_specs = P(None, ("grp", "gx"), None)
    return jax.shard_map(local, mesh=mesh, in_specs=in_specs, out_specs=out_specs, check_vma=False)
```

```python
import jax
import jax.numpy as jnp
import numpy as np
from jax import lax
from jax.experimental import pallas as pl
from jax.experimental.pallas import tpu as pltpu
from jax.sharding import PartitionSpec as P

BY = 8
BZ = 112
TS = 16
NT = 8
FIELDS = 4
ZB = 16

epsilon = 1e-05
sharpness = 80.0
AXIS_ORDERS = np.array([[0, 1, 2], [0, 2, 1], [1, 0, 2], [1, 2, 0], [2, 0, 1], [2, 1, 0]], np.int32)


def extended(x, sides, width):
    for axis, dim in sides:
        size, length = (lax.axis_size(axis), x.shape[dim])
        up = [(i, (i + 1) % size) for i in range(size - 1)]
        down = [(j, i) for i, j in up]
        last = lax.slice_in_dim(x, length - width, length, axis=dim)
        leading = lax.slice_in_dim(x, 0, width, axis=dim)
        before = lax.ppermute(last, axis, up)
        after = lax.ppermute(leading, axis, down)
        x = jnp.concatenate([before, x, after], axis=dim)
    return x


def band_table(positions, targets, period):
    offset = (positions[:, None] - targets[None, :]) % period
    return (offset < TS).astype(jnp.float32)


def contract(letters, data, table):
    return jnp.einsum(letters, data, table, precision=lax.Precision.HIGHEST)


def expand(flag):
    return flag[:, None, None, None]


def gather_planes(bank, axis):
    size = lax.axis_size(axis)
    me = lax.axis_index(axis)
    held = bank[None]
    step = 1
    while step < size:
        radix = min(4, size // step)
        digit = (me // step) % radix
        blocks = [held] + [
            lax.ppermute(held, axis, [(i, i ^ (s * step)) for i in range(size)]) for s in range(1, radix)
        ]
        placed = []
        for d in range(radix):
            value = jnp.zeros_like(held)
            for s in range(radix):
                value = value + jnp.where((digit ^ s) == d, blocks[s], 0.0)
            placed.append(value)
        held = jnp.concatenate(placed, 0)
        step *= radix
    return held


def rotated_kernels(planes, orient, bank_id):
    count = planes.shape[1]
    picked = jnp.zeros((orient.shape[0], TS, TS, TS), jnp.float32)
    for m in range(count):
        base = planes[:, m, :].reshape(TS, TS, TS)
        picked = picked + jnp.where(expand(bank_id == m), base[None], 0.0)
    flips = orient % 8
    for axis_num in range(3):
        bit = (flips // 2**axis_num) % 2 == 1
        picked = jnp.where(expand(bit), jnp.flip(picked, axis=axis_num + 1), picked)
    order_row = orient // 8
    rotated = jnp.zeros_like(picked)
    for row in range(AXIS_ORDERS.shape[0]):
        perm = (0,) + tuple(1 + int(p) for p in np.argsort(AXIS_ORDERS[row]))
        rotated = rotated + jnp.where(expand(order_row == row), jnp.transpose(picked, perm), 0.0)
    flat = rotated.reshape(rotated.shape[0], -1)
    centered = flat - jnp.mean(flat, axis=1, keepdims=True)
    norm = jnp.sqrt(jnp.sum(centered * centered, axis=1, keepdims=True) + epsilon)
    return (centered / norm).reshape(rotated.shape)


def toeplitz_rhs(kernels):
    nt = kernels.shape[0]
    per = nt // FIELDS
    dims = (TS + ZB, 2 * TS * nt, 2 * nt * ZB)
    w = lax.broadcasted_iota(jnp.int32, dims, 0)
    k = lax.broadcasted_iota(jnp.int32, dims, 1)
    n = lax.broadcasted_iota(jnp.int32, dims, 2)
    shift = ((w - n % ZB == k % TS) & (k // TS == n // ZB)).astype(jnp.float32)
    pairs = kernels.reshape(FIELDS, per, TS // 2, 2, TS, TS)
    kt = jnp.transpose(pairs, (2, 4, 3, 1, 0, 5)).reshape(TS * TS // 2, 2 * TS * nt)
    rhs = jnp.einsum("rk,wkn->rwn", kt, shift, precision=lax.Precision.HIGHEST)
    return rhs.reshape(TS // 2, 1, TS * (TS + ZB), 2 * nt * ZB)


def im2col_kernel(p_ref, o_ref):
    def body(y, carry):
        for zb in range(o_ref.shape[0]):
            for b in range(TS):
                o_ref[zb, y, :, b * (TS + ZB):(b + 1) * (TS + ZB)] = p_ref[y + b, :, zb * ZB: zb * ZB + TS + ZB]
        return carry
    lax.fori_loop(0, BY, body, 0)


def im2col(padded_t, blocks):
    rows = padded_t.shape[1]
    return pl.pallas_call(
        im2col_kernel,
        out_shape=jax.ShapeDtypeStruct((blocks, BY, rows, TS * (TS + ZB)), jnp.float32),
        in_specs=[pl.BlockSpec(memory_space=pltpu.VMEM)],
        out_specs=pl.BlockSpec(memory_space=pltpu.VMEM),
        cost_estimate=pl.CostEstimate(flops=0, transcendentals=0, bytes_accessed=4 * blocks * BY * rows * TS * (TS + ZB)),
    )(padded_t)


def local(volume, bank, orient, bank_id, counts):
    rows_x = volume.shape[0]
    half = TS // 2
    nt = orient.shape[0]
    grid = volume.reshape(rows_x, BY, BZ)
    len_x = rows_x + TS
    len_y = BY + TS
    len_z = BZ + TS
    blocks = BZ // ZB
    planes = gather_planes(bank, "gx")
    per = nt // FIELDS
    kernels = rotated_kernels(planes, orient, bank_id)
    rhs = toeplitz_rhs(kernels)
    field_in = extended(grid, (("gx", 0),), half)
    padded = jnp.pad(field_in, ((0, 0), (half, TS - half), (half, TS - half)))
    cols = im2col(jnp.transpose(padded[: len_x - 1], (1, 0, 2)), blocks)
    cols = cols.reshape(1, blocks * BY, len_x - 1, TS * (TS + ZB))
    both = lax.conv_general_dilated(
        cols, rhs, (1, 1), "VALID", rhs_dilation=(2, 1),
        dimension_numbers=lax.ConvDimensionNumbers((0, 3, 2, 1), (3, 2, 0, 1), (0, 3, 1, 2)),
        precision=lax.Precision.HIGH,
    )
    numer = both[:, :rows_x, :, : nt * ZB] + both[:, 1:, :, nt * ZB:]
    numer = numer.reshape(rows_x, blocks * BY, nt * ZB)
    pos_x = jnp.arange(len_x, dtype=jnp.int32)
    out_x = jnp.arange(rows_x, dtype=jnp.int32)
    pos_y = half + jnp.arange(BY, dtype=jnp.int32)
    pos_z = half + jnp.arange(BZ, dtype=jnp.int32)
    squares = field_in * field_in
    energy = contract(
        "xyz,zn->xyn", squares, band_table(pos_z, jnp.arange(BZ, dtype=jnp.int32), len_z)
    )
    energy = contract(
        "xyn,ym->xmn", energy, band_table(pos_y, jnp.arange(BY, dtype=jnp.int32), len_y)
    )
    energy = contract("xmn,xl->lmn", energy, band_table(pos_x, out_x, len_x))
    energy = jnp.transpose(energy.reshape(rows_x, BY, blocks, ZB), (0, 2, 1, 3))
    energy = jnp.tile(energy.reshape(rows_x, blocks * BY, ZB), (1, 1, nt))
    scores = numer / jnp.sqrt(energy + epsilon)
    weights = jnp.transpose(counts.astype(jnp.float32).reshape(FIELDS, per)).reshape(nt)
    weighted = jnp.repeat(weights, ZB)[None, None] * jnp.exp(sharpness * scores)
    half_lanes = FIELDS * ZB
    grouped = weighted[:, :, :half_lanes]
    for p in range(1, per):
        grouped = grouped + weighted[:, :, p * half_lanes:(p + 1) * half_lanes]
    totals = weights[:FIELDS]
    for p in range(1, per):
        totals = totals + weights[p * FIELDS:(p + 1) * FIELDS]
    fields = jnp.log(grouped / jnp.repeat(totals, ZB)[None, None])
    planes_out = []
    for k in range(FIELDS):
        one = fields[:, :, k * ZB:(k + 1) * ZB].reshape(rows_x, blocks, BY, ZB)
        planes_out.append(jnp.transpose(one, (0, 2, 1, 3)).reshape(rows_x, BY * BZ))
    return jnp.stack(planes_out)


def solution(mesh):
    in_specs = (P(("grp", "gx"), None), P(None, "gx"), P(), P(), P())
    out_specs = P(None, ("grp", "gx"), None)
    return jax.shard_map(local, mesh=mesh, in_specs=in_specs, out_specs=out_specs, check_vma=False)
```

```python
import jax
import jax.numpy as jnp
import numpy as np
from jax import lax
from jax.experimental import pallas as pl
from jax.experimental.pallas import tpu as pltpu
from jax.sharding import PartitionSpec as P

BY = 8
BZ = 112
TS = 16
NT = 8
FIELDS = 4
ZB = 16

epsilon = 1e-05
sharpness = 80.0
AXIS_ORDERS = np.array([[0, 1, 2], [0, 2, 1], [1, 0, 2], [1, 2, 0], [2, 0, 1], [2, 1, 0]], np.int32)


def extended(x, sides, width):
    for axis, dim in sides:
        size, length = (lax.axis_size(axis), x.shape[dim])
        up = [(i, (i + 1) % size) for i in range(size - 1)]
        down = [(j, i) for i, j in up]
        last = lax.slice_in_dim(x, length - width, length, axis=dim)
        leading = lax.slice_in_dim(x, 0, width, axis=dim)
        before = lax.ppermute(last, axis, up)
        after = lax.ppermute(leading, axis, down)
        x = jnp.concatenate([before, x, after], axis=dim)
    return x


def band_table(positions, targets, period):
    offset = (positions[:, None] - targets[None, :]) % period
    return (offset < TS).astype(jnp.float32)


def contract(letters, data, table):
    return jnp.einsum(letters, data, table, precision=lax.Precision.HIGH)


def expand(flag):
    return flag[:, None, None, None]


def gather_planes(bank, axis):
    size = lax.axis_size(axis)
    me = lax.axis_index(axis)
    held = bank[None]
    step = 1
    while step < size:
        radix = min(4, size // step)
        digit = (me // step) % radix
        blocks = [held] + [
            lax.ppermute(held, axis, [(i, i ^ (s * step)) for i in range(size)]) for s in range(1, radix)
        ]
        placed = []
        for d in range(radix):
            value = jnp.zeros_like(held)
            for s in range(radix):
                value = value + jnp.where((digit ^ s) == d, blocks[s], 0.0)
            placed.append(value)
        held = jnp.concatenate(placed, 0)
        step *= radix
    return held


def rotated_kernels(planes, orient, bank_id):
    count = planes.shape[1]
    picked = jnp.zeros((orient.shape[0], TS, TS, TS), jnp.float32)
    for m in range(count):
        base = planes[:, m, :].reshape(TS, TS, TS)
        picked = picked + jnp.where(expand(bank_id == m), base[None], 0.0)
    flips = orient % 8
    for axis_num in range(3):
        bit = (flips // 2**axis_num) % 2 == 1
        picked = jnp.where(expand(bit), jnp.flip(picked, axis=axis_num + 1), picked)
    order_row = orient // 8
    rotated = jnp.zeros_like(picked)
    for row in range(AXIS_ORDERS.shape[0]):
        perm = (0,) + tuple(1 + int(p) for p in np.argsort(AXIS_ORDERS[row]))
        rotated = rotated + jnp.where(expand(order_row == row), jnp.transpose(picked, perm), 0.0)
    flat = rotated.reshape(rotated.shape[0], -1)
    centered = flat - jnp.mean(flat, axis=1, keepdims=True)
    norm = jnp.sqrt(jnp.sum(centered * centered, axis=1, keepdims=True) + epsilon)
    return (centered / norm).reshape(rotated.shape)


def toeplitz_rhs(kernels):
    nt = kernels.shape[0]
    per = nt // FIELDS
    dims = (TS + ZB, 2 * TS * nt, 2 * nt * ZB)
    w = lax.broadcasted_iota(jnp.int32, dims, 0)
    k = lax.broadcasted_iota(jnp.int32, dims, 1)
    n = lax.broadcasted_iota(jnp.int32, dims, 2)
    shift = ((w - n % ZB == k % TS) & (k // TS == n // ZB)).astype(jnp.float32)
    pairs = kernels.reshape(FIELDS, per, TS // 2, 2, TS, TS)
    kt = jnp.transpose(pairs, (2, 4, 3, 1, 0, 5)).reshape(TS * TS // 2, 2 * TS * nt)
    rhs = jnp.einsum("rk,wkn->rwn", kt, shift, precision=lax.Precision.HIGHEST)
    return rhs.reshape(TS // 2, 1, TS * (TS + ZB), 2 * nt * ZB)


def im2col_kernel(p_ref, o_ref):
    def body(y, carry):
        for zb in range(o_ref.shape[0]):
            for b in range(TS):
                o_ref[zb, y, :, b * (TS + ZB):(b + 1) * (TS + ZB)] = p_ref[y + b, :, zb * ZB: zb * ZB + TS + ZB]
        return carry
    lax.fori_loop(0, BY, body, 0)


def im2col(padded_t, blocks):
    rows = padded_t.shape[1]
    return pl.pallas_call(
        im2col_kernel,
        out_shape=jax.ShapeDtypeStruct((blocks, BY, rows, TS * (TS + ZB)), jnp.float32),
        in_specs=[pl.BlockSpec(memory_space=pltpu.VMEM)],
        out_specs=pl.BlockSpec(memory_space=pltpu.VMEM),
        cost_estimate=pl.CostEstimate(flops=0, transcendentals=0, bytes_accessed=4 * blocks * BY * rows * TS * (TS + ZB)),
    )(padded_t)


def local(volume, bank, orient, bank_id, counts):
    rows_x = volume.shape[0]
    half = TS // 2
    nt = orient.shape[0]
    grid = volume.reshape(rows_x, BY, BZ)
    len_x = rows_x + TS
    len_y = BY + TS
    len_z = BZ + TS
    blocks = BZ // ZB
    planes = gather_planes(bank, "gx")
    per = nt // FIELDS
    kernels = rotated_kernels(planes, orient, bank_id)
    rhs = toeplitz_rhs(kernels)
    field_in = extended(grid, (("gx", 0),), half)
    padded = jnp.pad(field_in, ((0, 0), (half, TS - half), (half, TS - half)))
    cols = im2col(jnp.transpose(padded[: len_x - 1], (1, 0, 2)), blocks)
    cols = cols.reshape(1, blocks * BY, len_x - 1, TS * (TS + ZB))
    both = lax.conv_general_dilated(
        cols, rhs, (1, 1), "VALID", rhs_dilation=(2, 1),
        dimension_numbers=lax.ConvDimensionNumbers((0, 3, 2, 1), (3, 2, 0, 1), (0, 3, 1, 2)),
        precision=lax.Precision.HIGH,
    )
    numer = both[:, :rows_x, :, : nt * ZB] + both[:, 1:, :, nt * ZB:]
    numer = numer.reshape(rows_x, blocks * BY, nt * ZB)
    pos_x = jnp.arange(len_x, dtype=jnp.int32)
    out_x = jnp.arange(rows_x, dtype=jnp.int32)
    pos_y = half + jnp.arange(BY, dtype=jnp.int32)
    pos_z = half + jnp.arange(BZ, dtype=jnp.int32)
    squares = field_in * field_in
    energy = contract(
        "xyz,zn->xyn", squares, band_table(pos_z, jnp.arange(BZ, dtype=jnp.int32), len_z)
    )
    energy = contract(
        "xyn,ym->xmn", energy, band_table(pos_y, jnp.arange(BY, dtype=jnp.int32), len_y)
    )
    energy = contract("xmn,xl->lmn", energy, band_table(pos_x, out_x, len_x))
    energy = jnp.transpose(energy.reshape(rows_x, BY, blocks, ZB), (0, 2, 1, 3))
    energy = jnp.tile(energy.reshape(rows_x, blocks * BY, ZB), (1, 1, nt))
    scores = numer / jnp.sqrt(energy + epsilon)
    weights = jnp.transpose(counts.astype(jnp.float32).reshape(FIELDS, per)).reshape(nt)
    weighted = jnp.repeat(weights, ZB)[None, None] * jnp.exp(sharpness * scores)
    half_lanes = FIELDS * ZB
    grouped = weighted[:, :, :half_lanes]
    for p in range(1, per):
        grouped = grouped + weighted[:, :, p * half_lanes:(p + 1) * half_lanes]
    totals = weights[:FIELDS]
    for p in range(1, per):
        totals = totals + weights[p * FIELDS:(p + 1) * FIELDS]
    fields = jnp.log(grouped / jnp.repeat(totals, ZB)[None, None])
    planes_out = []
    for k in range(FIELDS):
        one = fields[:, :, k * ZB:(k + 1) * ZB].reshape(rows_x, blocks, BY, ZB)
        planes_out.append(jnp.transpose(one, (0, 2, 1, 3)).reshape(rows_x, BY * BZ))
    return jnp.stack(planes_out)


def solution(mesh):
    in_specs = (P(("grp", "gx"), None), P(None, "gx"), P(), P(), P())
    out_specs = P(None, ("grp", "gx"), None)
    return jax.shard_map(local, mesh=mesh, in_specs=in_specs, out_specs=out_specs, check_vma=False)
```

```python
import jax
import jax.numpy as jnp
import numpy as np
from jax import lax
from jax.experimental import pallas as pl
from jax.experimental.pallas import tpu as pltpu
from jax.sharding import PartitionSpec as P

BY = 8
BZ = 112
TS = 16
NT = 8
FIELDS = 4
ZB = 16

epsilon = 1e-05
sharpness = 80.0
AXIS_ORDERS = np.array([[0, 1, 2], [0, 2, 1], [1, 0, 2], [1, 2, 0], [2, 0, 1], [2, 1, 0]], np.int32)


def extended(x, sides, width):
    for axis, dim in sides:
        size, length = (lax.axis_size(axis), x.shape[dim])
        up = [(i, (i + 1) % size) for i in range(size - 1)]
        down = [(j, i) for i, j in up]
        last = lax.slice_in_dim(x, length - width, length, axis=dim)
        leading = lax.slice_in_dim(x, 0, width, axis=dim)
        before = lax.ppermute(last, axis, up)
        after = lax.ppermute(leading, axis, down)
        x = jnp.concatenate([before, x, after], axis=dim)
    return x


def band_table(positions, targets, period):
    offset = (positions[:, None] - targets[None, :]) % period
    return (offset < TS).astype(jnp.float32)


def contract(letters, data, table):
    return jnp.einsum(letters, data, table, precision=lax.Precision.HIGHEST)


def expand(flag):
    return flag[:, None, None, None]


def gather_planes(bank, axis):
    size = lax.axis_size(axis)
    me = lax.axis_index(axis)
    held = bank[None]
    step = 1
    while step < size:
        radix = min(4, size // step)
        digit = (me // step) % radix
        blocks = [held] + [
            lax.ppermute(held, axis, [(i, i ^ (s * step)) for i in range(size)]) for s in range(1, radix)
        ]
        placed = []
        for d in range(radix):
            value = jnp.zeros_like(held)
            for s in range(radix):
                value = value + jnp.where((digit ^ s) == d, blocks[s], 0.0)
            placed.append(value)
        held = jnp.concatenate(placed, 0)
        step *= radix
    return held


def rotated_kernels(planes, orient, bank_id):
    count = planes.shape[1]
    picked = jnp.zeros((orient.shape[0], TS, TS, TS), jnp.float32)
    for m in range(count):
        base = planes[:, m, :].reshape(TS, TS, TS)
        picked = picked + jnp.where(expand(bank_id == m), base[None], 0.0)
    flips = orient % 8
    for axis_num in range(3):
        bit = (flips // 2**axis_num) % 2 == 1
        picked = jnp.where(expand(bit), jnp.flip(picked, axis=axis_num + 1), picked)
    order_row = orient // 8
    rotated = jnp.zeros_like(picked)
    for row in range(AXIS_ORDERS.shape[0]):
        perm = (0,) + tuple(1 + int(p) for p in np.argsort(AXIS_ORDERS[row]))
        rotated = rotated + jnp.where(expand(order_row == row), jnp.transpose(picked, perm), 0.0)
    flat = rotated.reshape(rotated.shape[0], -1)
    centered = flat - jnp.mean(flat, axis=1, keepdims=True)
    norm = jnp.sqrt(jnp.sum(centered * centered, axis=1, keepdims=True) + epsilon)
    return (centered / norm).reshape(rotated.shape)


def toeplitz_rhs(kernels):
    nt = kernels.shape[0]
    per = nt // FIELDS
    dims = (TS + ZB, 2 * TS * nt, 2 * nt * ZB)
    w = lax.broadcasted_iota(jnp.int32, dims, 0)
    k = lax.broadcasted_iota(jnp.int32, dims, 1)
    n = lax.broadcasted_iota(jnp.int32, dims, 2)
    shift = ((w - n % ZB == k % TS) & (k // TS == n // ZB)).astype(jnp.float32)
    pairs = kernels.reshape(FIELDS, per, TS // 2, 2, TS, TS)
    kt = jnp.transpose(pairs, (2, 4, 3, 1, 0, 5)).reshape(TS * TS // 2, 2 * TS * nt)
    rhs = jnp.einsum("rk,wkn->rwn", kt, shift, precision=lax.Precision.HIGHEST)
    return rhs.reshape(TS // 2, 1, TS * (TS + ZB), 2 * nt * ZB)


def im2col_kernel(p_ref, o_ref):
    def body(y, carry):
        for zb in range(o_ref.shape[0]):
            pieces = [p_ref[y + b, :, zb * ZB: zb * ZB + TS + ZB] for b in range(TS)]
            o_ref[zb, y, :, :] = jnp.concatenate(pieces, axis=-1)
        return carry
    lax.fori_loop(0, BY, body, 0)


def im2col(padded_t, blocks):
    rows = padded_t.shape[1]
    return pl.pallas_call(
        im2col_kernel,
        out_shape=jax.ShapeDtypeStruct((blocks, BY, rows, TS * (TS + ZB)), jnp.float32),
        in_specs=[pl.BlockSpec(memory_space=pltpu.VMEM)],
        out_specs=pl.BlockSpec(memory_space=pltpu.VMEM),
        cost_estimate=pl.CostEstimate(flops=0, transcendentals=0, bytes_accessed=4 * blocks * BY * rows * TS * (TS + ZB)),
    )(padded_t)


def local(volume, bank, orient, bank_id, counts):
    rows_x = volume.shape[0]
    half = TS // 2
    nt = orient.shape[0]
    grid = volume.reshape(rows_x, BY, BZ)
    len_x = rows_x + TS
    len_y = BY + TS
    len_z = BZ + TS
    blocks = BZ // ZB
    planes = gather_planes(bank, "gx")
    per = nt // FIELDS
    kernels = rotated_kernels(planes, orient, bank_id)
    rhs = toeplitz_rhs(kernels)
    field_in = extended(grid, (("gx", 0),), half)
    padded = jnp.pad(field_in, ((0, 0), (half, TS - half), (half, TS - half)))
    cols = im2col(jnp.transpose(padded[: len_x - 1], (1, 0, 2)), blocks)
    cols = cols.reshape(1, blocks * BY, len_x - 1, TS * (TS + ZB))
    both = lax.conv_general_dilated(
        cols, rhs, (1, 1), "VALID", rhs_dilation=(2, 1),
        dimension_numbers=lax.ConvDimensionNumbers((0, 3, 2, 1), (3, 2, 0, 1), (0, 3, 1, 2)),
        precision=lax.Precision.HIGH,
    )
    numer = both[:, :rows_x, :, : nt * ZB] + both[:, 1:, :, nt * ZB:]
    numer = numer.reshape(rows_x, blocks * BY, nt * ZB)
    pos_x = jnp.arange(len_x, dtype=jnp.int32)
    out_x = jnp.arange(rows_x, dtype=jnp.int32)
    pos_y = half + jnp.arange(BY, dtype=jnp.int32)
    pos_z = half + jnp.arange(BZ, dtype=jnp.int32)
    squares = field_in * field_in
    energy = contract(
        "xyz,zn->xyn", squares, band_table(pos_z, jnp.arange(BZ, dtype=jnp.int32), len_z)
    )
    energy = contract(
        "xyn,ym->xmn", energy, band_table(pos_y, jnp.arange(BY, dtype=jnp.int32), len_y)
    )
    energy = contract("xmn,xl->lmn", energy, band_table(pos_x, out_x, len_x))
    energy = jnp.transpose(energy.reshape(rows_x, BY, blocks, ZB), (0, 2, 1, 3))
    energy = jnp.tile(energy.reshape(rows_x, blocks * BY, ZB), (1, 1, nt))
    scores = numer / jnp.sqrt(energy + epsilon)
    weights = jnp.transpose(counts.astype(jnp.float32).reshape(FIELDS, per)).reshape(nt)
    weighted = jnp.repeat(weights, ZB)[None, None] * jnp.exp(sharpness * scores)
    half_lanes = FIELDS * ZB
    grouped = weighted[:, :, :half_lanes]
    for p in range(1, per):
        grouped = grouped + weighted[:, :, p * half_lanes:(p + 1) * half_lanes]
    totals = weights[:FIELDS]
    for p in range(1, per):
        totals = totals + weights[p * FIELDS:(p + 1) * FIELDS]
    fields = jnp.log(grouped / jnp.repeat(totals, ZB)[None, None])
    planes_out = []
    for k in range(FIELDS):
        one = fields[:, :, k * ZB:(k + 1) * ZB].reshape(rows_x, blocks, BY, ZB)
        planes_out.append(jnp.transpose(one, (0, 2, 1, 3)).reshape(rows_x, BY * BZ))
    return jnp.stack(planes_out)


def solution(mesh):
    in_specs = (P(("grp", "gx"), None), P(None, "gx"), P(), P(), P())
    out_specs = P(None, ("grp", "gx"), None)
    return jax.shard_map(local, mesh=mesh, in_specs=in_specs, out_specs=out_specs, check_vma=False)
```
